128 devices in a mesh: seq: 8 (over z, core), exp: 16 (over y, x).
Axes of the slice: x: 4, y: 4, z: 4, core: 2. Of those that a mesh axis runs over, the one named last changes fastest.
Arguments:
- tokens: bfloat16 [16, 1024, 2048], P('exp', 'seq'), may hold values from -6 to 6
- in_gain: float32 [2048], replicated, may hold values from 0.1 to 1.9
- post_gain: float32 [2048], replicated, may hold values from 0.1 to 1.9
- w_query: bfloat16 [2048, 2048], P(None, 'seq'), may hold values from -0.125 to 0.125
- w_key: bfloat16 [2048, 2048], P(None, 'seq'), may hold values from -0.125 to 0.125
- w_value: bfloat16 [2048, 4096], P(None, 'seq'), may hold values from -0.125 to 0.125
- w_gate_out: bfloat16 [2048, 4096], P(None, 'seq'), may hold values from -0.125 to 0.125
- w_rates: bfloat16 [2048, 64], replicated, may hold values from -0.125 to 0.125
- conv_query: float32 [4, 2048], P(None, 'seq'), may hold values from -0.5 to 0.5
- conv_key: float32 [4, 2048], P(None, 'seq'), may hold values from -0.5 to 0.5
- conv_value: float32 [4, 4096], P(None, 'seq'), may hold values from -0.5 to 0.5
- decay_rate: float32 [32], P('seq'), may hold values from 1e-05 to 0.1
- time_bias: float32 [32], P('seq'), may hold values from -4 to 4
- head_gain: float32 [128], replicated, may hold values from 0.1 to 1.9
- w_out: bfloat16 [4096, 2048], P('seq'), may hold values from -0.25 to 0.25
- expert_ids: int32 [16, 1024, 10], P('exp', 'seq'), may hold values from 0 to 255, all different within a row; in each aligned block of 128 rows (0 to 127, 128 to 255, ..., all dimensions but the last counted through in order) at most 6 rows name the same one
- route_gates: float32 [16, 1024, 10], P('exp', 'seq'), may hold values from 0.05 to 0.6
- w_expert_gate: bfloat16 [256, 2048, 512], P(('seq', 'exp')), may hold values from -0.125 to 0.125
- w_expert_up: bfloat16 [256, 2048, 512], P(('seq', 'exp')), may hold values from -0.125 to 0.125
- w_expert_down: bfloat16 [256, 512, 2048], P(('seq', 'exp')), may hold values from -0.25 to 0.25
Outputs:
- mixed: bfloat16 [16, 1024, 2048], P('exp', 'seq')
The draws below stay inside these ranges and needn't reach their ends.
Inputs may be any that keep to these rules, and one draw needn't show every extreme that they name: `expert_ids`: each token names 10 different experts. Within the tokens of one device (aligned blocks of 128 rows in sequence order) no expert is named by more than 6 rows, a bound that some block reaches.
All inputs are finite; a program needn't handle non-finite values.
Results may differ from the reference program's by a relative error of at most 0.02.
Values may be sent and summed in bfloat16 or wider, within the bound.
No kernel may reach another device: no remote copies, remote signals or barrier semaphores. Data moves between devices by JAX's collectives and lax.ppermute only.
A program may use at most 128 MiB of HBM per device.

```python
import math
import jax
import jax.numpy as jnp
import numpy as np
from jax import lax

D = 2048
NV = 32
NK = 16
DK = 128
DV = 128
CONV = 4
CH = 64
FFE = 512
TOP = 10
TOK_DEV = 128
SEG = 1024
LEN = 16384
VGROUP = 4
EXPERTS = 256
CAP = 6
N_EXP = 16


def level_of(key, dims, split, low, largest):
    level = 1.0
    for axis_at, parts in split:
        steps = jax.random.uniform(jax.random.fold_in(jax.random.fold_in(key, 6), axis_at), (parts,), jnp.float32, low / len(split), largest / len(split))
        level = level * jnp.repeat(jnp.exp(steps), dims[axis_at] // parts).reshape((-1,) + (1,) * (len(dims) - 1 - axis_at))
    return level


def routed_block(rng, own, number, rows, number_of, top, reach, skew):
    sequence = jax.random.permutation(rng, number_of)
    crowded, common = shares(number_of, rows * top, reach, skew, True), shares(number_of, rows * top, reach, skew, False)
    places = jnp.arange(number_of)

    def named(sizes, turn):
        used = int((sizes > 0).sum())
        fixed = max(1, used // 4)
        moved = fixed + (places - fixed + turn * (used - fixed)) % max(1, number_of - fixed)
        return jnp.zeros((number_of,), jnp.int32).at[sequence[jnp.where(places < fixed, places, moved)]].set(jnp.asarray(sizes, jnp.int32))

    sizes = jnp.where(number % 4 == 0, named(crowded, number // 4), named(common, number - number // 4 - 1))
    mixed = jax.random.permutation(jax.random.fold_in(own, 3), number_of)
    source_of, sink = mixed[0:number_of // 2 * 2:2], mixed[1:number_of // 2 * 2:2]
    slack = jnp.minimum(sizes[source_of] - 1, reach - sizes[sink]) // 2
    slack = jnp.where((source_of == sequence[0]) | (sink == sequence[0]) | (sizes[sink] == 0), 0, jnp.maximum(slack, 0))
    moved = jax.random.randint(jax.random.fold_in(own, 4), (number_of // 2,), 0, 1 << 20) % (slack + 1)
    sizes = sizes.at[source_of].add(-moved).at[sink].add(moved)
    items = jnp.searchsorted(jnp.cumsum(sizes), jnp.arange(rows * top), side="right").astype(jnp.int32)
    listing = items.reshape(top, rows).T
    listing = listing[jax.random.permutation(jax.random.fold_in(own, 1), rows)]
    turn = jax.random.randint(jax.random.fold_in(own, 2), (rows, 1), 0, top)
    return jnp.take_along_axis(listing, (jnp.arange(top)[None, :] + turn) % top, axis=1)


def shares(amount, total, reach, skew, full):
    portions = [(1 << 20) // math.isqrt(standing ** skew) + 1 for standing in range(1, amount + 1)]
    largest = reach if full else min(reach, max(-(-total // amount), total * portions[0] // sum(portions)))
    least = 1 if total - largest >= amount - 1 else 0
    holding, spare = [largest] + [least] * (amount - 1), total - largest - least * (amount - 1)
    while spare > 0:
        movable = [i for i in range(1, amount) if holding[i] < largest] or [i for i in range(1, amount) if holding[i] < reach]
        pool, remaining = sum([portions[i] for i in movable]), spare
        for i in movable:
            addition = min(reach - holding[i], max(1, remaining * portions[i] // pool), spare)
            holding[i] = holding[i] + addition
            spare = spare - addition
    return np.array(holding)


def noise(key, shape, width, bound, shards=(), kind=jnp.bfloat16):
    drawn = jax.random.normal(key, shape, jnp.float32) * width
    if len(shards) > 0:
        drawn = level_of(key, shape, shards, -0.22, 0.18) * drawn
    return jnp.clip(drawn, min=-bound, max=bound).astype(kind)


def setup_inputs(seed: int = 0) -> dict:
    arg_keys = jax.random.split(jax.random.key(seed), 21)
    tokens = noise(arg_keys[0], (N_EXP, SEG, D), 1.0, 6.0, ((0, 16), (1, 8)))
    in_gain = jnp.clip(1.0 + 0.18 * jax.random.normal(arg_keys[1], (D,), jnp.float32), 0.1, 1.9)
    post_gain = jnp.clip(1.0 + 0.18 * jax.random.normal(arg_keys[2], (D,), jnp.float32), 0.1, 1.9)
    w_query = noise(arg_keys[3], (D, NK * DK), D ** -0.5, 0.125, ((1, 8),))
    w_key = noise(arg_keys[4], (D, NK * DK), D ** -0.5, 0.125, ((1, 8),))
    w_value = noise(arg_keys[5], (D, NV * DV), D ** -0.5, 0.125, ((1, 8),))
    w_gate_out = noise(arg_keys[6], (D, NV * DV), D ** -0.5, 0.125, ((1, 8),))
    w_rates = noise(arg_keys[7], (D, 2 * NV), D ** -0.5, 0.125)
    conv_query = jnp.clip(jax.random.uniform(arg_keys[8], (CONV, NK * DK), jnp.float32, -0.5, 0.5) * level_of(arg_keys[8], (CONV, NK * DK), ((1, 8),), -0.4, 0.0), -0.5, 0.5)
    conv_key = jnp.clip(jax.random.uniform(arg_keys[9], (CONV, NK * DK), jnp.float32, -0.5, 0.5) * level_of(arg_keys[9], (CONV, NK * DK), ((1, 8),), -0.4, 0.0), -0.5, 0.5)
    conv_value = jnp.clip(jax.random.uniform(arg_keys[10], (CONV, NV * DV), jnp.float32, -0.5, 0.5) * level_of(arg_keys[10], (CONV, NV * DV), ((1, 8),), -0.4, 0.0), -0.5, 0.5)
    decay_rate = jnp.clip(jnp.exp(math.log(0.1) - 9.2103404 * jax.random.uniform(arg_keys[11], (NV,), jnp.float32) ** level_of(arg_keys[11], (NV,), ((0, 8),), -0.2, 0.2)), 9.999999747378752e-06, 0.1)
    time_bias = noise(arg_keys[12], (NV,), 1.5, 4.0, ((0, 8),), jnp.float32)
    head_gain = jnp.clip(1.0 + 0.18 * jax.random.normal(arg_keys[13], (DV,), jnp.float32), 0.1, 1.9)
    w_out = noise(arg_keys[14], (NV * DV, D), (NV * DV // 8) ** -0.5, 0.25, ((0, 8),))
    expert_ids_keys = jax.random.split(jax.random.fold_in(arg_keys[15], 1), N_EXP * SEG // TOK_DEV)
    expert_ids_turns = jax.random.permutation(jax.random.fold_in(arg_keys[15], 3), N_EXP * SEG // TOK_DEV)
    expert_ids = jax.vmap(lambda own, number: routed_block(jax.random.fold_in(arg_keys[15], 2), own, number, TOK_DEV, EXPERTS, TOP, CAP, 2))(expert_ids_keys, expert_ids_turns).reshape((N_EXP, SEG, TOP))
    route_gates = jnp.clip(jnp.exp(math.log(0.6) - 2.4849067 * jax.random.uniform(arg_keys[16], (N_EXP, SEG, TOP), jnp.float32) ** level_of(arg_keys[16], (N_EXP, SEG, TOP), ((0, 16), (1, 8)), -0.2, 0.2)), 0.05, 0.6)
    w_expert_gate = noise(arg_keys[17], (EXPERTS, D, FFE), D ** -0.5, 0.125, ((0, 128),))
    w_expert_up = noise(arg_keys[18], (EXPERTS, D, FFE), D ** -0.5, 0.125, ((0, 128),))
    w_expert_down = noise(arg_keys[19], (EXPERTS, FFE, D), FFE ** -0.5, 0.25, ((0, 128),))
    return dict(tokens=tokens, in_gain=in_gain, post_gain=post_gain, w_query=w_query, w_key=w_key, w_value=w_value, w_gate_out=w_gate_out, w_rates=w_rates, conv_query=conv_query, conv_key=conv_key, conv_value=conv_value, decay_rate=decay_rate, time_bias=time_bias, head_gain=head_gain, w_out=w_out, expert_ids=expert_ids, route_gates=route_gates, w_expert_gate=w_expert_gate, w_expert_up=w_expert_up, w_expert_down=w_expert_down)


EPSILON = 1e-06
HIGHEST = lax.Precision.HIGHEST

def scale_rows(values, row_gain):
    factor = lax.rsqrt(lax.optimization_barrier(jnp.mean(values * values, axis=-1, keepdims=True)) + EPSILON)
    return values * factor * row_gain

def causal_conv(projected, before, weights):
    taps = weights.shape[0]
    length = projected.shape[0]
    padded = jnp.concatenate([before, projected], axis=0)
    summed = weights[0] * projected
    for lag_index in range(1, taps):
        begin = taps - 1 - lag_index
        summed = summed + weights[lag_index] * padded[begin:begin + length]
    return jax.nn.silu(summed)

def unit_heads(values, head_count):
    shaped = values.reshape(values.shape[0], head_count, values.shape[1] // head_count)
    return shaped * lax.rsqrt(lax.optimization_barrier(jnp.sum(shaped * shaped, axis=-1, keepdims=True)) + EPSILON)

def span_parts(queries, key_vecs, value_vecs, beta_rates, decays):
    span_len = queries.shape[1]
    key_width = key_vecs.shape[2]
    cumulative = jnp.cumsum(decays, axis=1)
    lower_mask = jnp.tril(jnp.ones((span_len, span_len), dtype=bool))
    strict = jnp.tril(jnp.ones((span_len, span_len), dtype=bool), -1)
    spread = cumulative[:, :, None] - cumulative[:, None, :]
    fading = jnp.where(lower_mask, jnp.exp(jnp.where(lower_mask, spread, 0.0)), 0.0)
    key_dots = jnp.einsum('nik,njk->nij', key_vecs, key_vecs, precision=HIGHEST)
    system = jnp.where(strict, beta_rates[:, :, None] * key_dots * fading, 0.0) + jnp.eye(span_len, dtype=jnp.float32)
    targets = jnp.concatenate([(beta_rates * jnp.exp(cumulative))[:, :, None] * key_vecs, beta_rates[:, :, None] * value_vecs], axis=2)
    solved = lax.linalg.triangular_solve(system, targets, left_side=True, lower=True, unit_diagonal=True)
    key_mix = solved[:, :, :key_width]
    value_mix = solved[:, :, key_width:]
    query_fade = jnp.exp(cumulative)[:, :, None] * queries
    scores = jnp.einsum('nik,njk->nij', queries, key_vecs, precision=HIGHEST) * fading
    ending = cumulative[:, -1]
    key_fade = jnp.exp(ending[:, None] - cumulative)[:, :, None] * key_vecs
    return (query_fade, scores, key_mix, value_mix, key_fade, jnp.exp(ending))

def output_step(carried, pieces):
    query_fade, scores, key_mix, value_mix, key_fade, end_fade = pieces
    new_values = value_mix - jnp.dot(key_mix, carried, precision=HIGHEST)
    output = jnp.dot(query_fade, carried, precision=HIGHEST) + jnp.dot(scores, new_values, precision=HIGHEST)
    carried = end_fade * carried + jnp.dot(key_fade.T, new_values, precision=HIGHEST)
    return (carried, output)

def to_spans(values):
    return values.reshape((values.shape[0] // CH, CH) + values.shape[1:])

def head_recurrence(inputs):
    queries, key_vecs, value_vecs, beta_rates, decays = inputs
    pieces = span_parts(to_spans(queries), to_spans(key_vecs), to_spans(value_vecs), to_spans(beta_rates), to_spans(decays))
    zero_state = jnp.zeros((queries.shape[1], value_vecs.shape[1]), jnp.float32)
    outputs = lax.scan(output_step, zero_state, pieces)[1]
    return outputs.reshape(queries.shape[0], value_vecs.shape[1])

def block_places(block_ids):
    columns = jnp.arange(EXPERTS, dtype=jnp.int32)
    onehot = (block_ids[:, None] == columns[None, :]).astype(jnp.int32)
    earlier = (jnp.cumsum(onehot, axis=0) - onehot).astype(jnp.int32)
    return lax.optimization_barrier(jnp.sum(earlier * onehot, axis=1)).astype(jnp.int32)

def reference(tokens, in_gain, post_gain, w_query, w_key, w_value, w_gate_out, w_rates, conv_query, conv_key, conv_value, decay_rate, time_bias, head_gain, w_out, expert_ids, route_gates, w_expert_gate, w_expert_up, w_expert_down):
    token_rows = tokens.reshape(LEN, D)
    normed = scale_rows(token_rows.astype(jnp.float32), in_gain).astype(jnp.bfloat16)
    rate_logits = jnp.dot(normed.astype(jnp.float32), w_rates.astype(jnp.float32), preferred_element_type=jnp.float32).astype(jnp.bfloat16)
    query_proj = jnp.dot(normed.astype(jnp.float32), w_query.astype(jnp.float32), preferred_element_type=jnp.float32)
    key_proj = jnp.dot(normed.astype(jnp.float32), w_key.astype(jnp.float32), preferred_element_type=jnp.float32)
    value_proj = jnp.dot(normed.astype(jnp.float32), w_value.astype(jnp.float32), preferred_element_type=jnp.float32)
    gate_proj = jnp.dot(normed.astype(jnp.float32), w_gate_out.astype(jnp.float32), preferred_element_type=jnp.float32)
    lag_rows = CONV - 1
    query_conv = causal_conv(query_proj, jnp.zeros((lag_rows, query_proj.shape[1]), jnp.float32), conv_query)
    key_conv = causal_conv(key_proj, jnp.zeros((lag_rows, key_proj.shape[1]), jnp.float32), conv_key)
    value_conv = causal_conv(value_proj, jnp.zeros((lag_rows, value_proj.shape[1]), jnp.float32), conv_value)
    ratio = NV // NK
    queries = jnp.repeat(unit_heads(query_conv, NK) * DK ** (-0.5), ratio, axis=1)
    key_vecs = jnp.repeat(unit_heads(key_conv, NK), ratio, axis=1)
    value_vecs = value_conv.reshape(LEN, NV, DV)
    rate_values = rate_logits.astype(jnp.float32)
    beta_rates = jax.nn.sigmoid(rate_values[:, :NV])
    decays = -decay_rate * jax.nn.softplus(rate_values[:, NV:] + time_bias)
    recurrent = lax.map(head_recurrence, (jnp.transpose(queries, (1, 0, 2)), jnp.transpose(key_vecs, (1, 0, 2)), jnp.transpose(value_vecs, (1, 0, 2)), beta_rates.T, decays.T))
    recurrent = jnp.transpose(recurrent, (1, 0, 2))
    gate_heads = gate_proj.reshape(LEN, NV, DV)
    gated = (scale_rows(recurrent, head_gain) * jax.nn.silu(gate_heads)).reshape(LEN, NV * DV).astype(jnp.bfloat16)
    group_cols = VGROUP * DV
    attended = jnp.zeros((LEN, D), jnp.float32)
    for group_index in range(NV // VGROUP):
        lo_col = group_index * group_cols
        partial_out = jnp.dot(gated[:, lo_col:lo_col + group_cols].astype(jnp.float32), w_out[lo_col:lo_col + group_cols].astype(jnp.float32), preferred_element_type=jnp.float32)
        attended = attended + lax.optimization_barrier(partial_out.astype(jnp.bfloat16)).astype(jnp.float32)
    residual = (token_rows.astype(jnp.float32) + attended).astype(jnp.bfloat16)
    moe_in = scale_rows(residual.astype(jnp.float32), post_gain).astype(jnp.bfloat16)
    blocks = LEN // TOK_DEV
    pair_ids = expert_ids.reshape(blocks, TOK_DEV * TOP).astype(jnp.int32)
    places = lax.map(block_places, pair_ids)
    token_index = (jnp.arange(LEN * TOP, dtype=jnp.int32) // TOP).reshape(blocks, TOK_DEV * TOP)
    block_index = jnp.broadcast_to(jnp.arange(blocks, dtype=jnp.int32)[:, None], pair_ids.shape)
    row_table = jnp.zeros((EXPERTS, blocks, CAP), jnp.int32).at[pair_ids, block_index, places].set(token_index)
    gate_table = jnp.zeros((EXPERTS, blocks, CAP), jnp.float32).at[pair_ids, block_index, places].set(route_gates.reshape(blocks, TOK_DEV * TOP))

    def one_expert(summed, inputs):
        row_index, gate_values, gate_weight, up_weight, down_weight = inputs
        flat_index = row_index.reshape(-1)
        picked = moe_in[flat_index]
        gate_part = jnp.dot(picked.astype(jnp.float32), gate_weight.astype(jnp.float32), preferred_element_type=jnp.float32)
        up_part = jnp.dot(picked.astype(jnp.float32), up_weight.astype(jnp.float32), preferred_element_type=jnp.float32)
        hidden = (jax.nn.silu(gate_part) * up_part).astype(jnp.bfloat16)
        expert_out = lax.optimization_barrier(jnp.dot(hidden.astype(jnp.float32), down_weight.astype(jnp.float32), preferred_element_type=jnp.float32).astype(jnp.bfloat16))
        summed = summed.at[flat_index].add(gate_values.reshape(-1)[:, None] * expert_out.astype(jnp.float32))
        return (summed, None)
    moe_sum = lax.scan(one_expert, jnp.zeros((LEN, D), jnp.float32), (row_table, gate_table, w_expert_gate, w_expert_up, w_expert_down))[0]
    mixed = (residual.astype(jnp.float32) + moe_sum).astype(jnp.bfloat16)
    return mixed.reshape(N_EXP, SEG, D)
```

```python
import jax
import jax.numpy as jnp
from jax import lax
from jax.sharding import PartitionSpec as P

DK = 128
DV = 128
CH = 64


EPSILON = 1e-06
HIGHEST = lax.Precision.HIGHEST


def scale_rows(values, row_gain):
    factor = lax.rsqrt(jnp.mean(values * values, axis=-1, keepdims=True) + EPSILON)
    return values * factor * row_gain


def causal_conv(projected, before, weights):
    taps = weights.shape[0]
    length = projected.shape[0]
    padded = jnp.concatenate([before, projected], axis=0)
    summed = weights[0] * projected
    for lag_index in range(1, taps):
        begin = taps - 1 - lag_index
        summed = summed + weights[lag_index] * padded[begin : begin + length]
    return jax.nn.silu(summed)


def unit_heads(values, head_count):
    shaped = values.reshape(values.shape[0], head_count, values.shape[1] // head_count)
    return shaped * lax.rsqrt(jnp.sum(shaped * shaped, axis=-1, keepdims=True) + EPSILON)


def mm(a, b):
    return jnp.matmul(a, b, precision=HIGHEST)


def unit_lower_inverse(strict_part):
    size = strict_part.shape[-1]
    power = -strict_part
    inverse = jnp.eye(size, dtype=jnp.float32) + power
    reach = 2
    while reach < size:
        power = mm(power, power)
        inverse = inverse + mm(inverse, power)
        reach *= 2
    return inverse


def chunk_parts(queries, key_vecs, value_vecs, beta_rates, decays):
    span_len = queries.shape[-2]
    cumulative = jnp.cumsum(decays, axis=-1)
    lower_mask = jnp.tril(jnp.ones((span_len, span_len), dtype=bool))
    strict = jnp.tril(jnp.ones((span_len, span_len), dtype=bool), -1)
    spread = cumulative[..., :, None] - cumulative[..., None, :]
    fading = jnp.where(lower_mask, jnp.exp(jnp.where(lower_mask, spread, 0.0)), 0.0)
    key_dots = jnp.einsum("...ik,...jk->...ij", key_vecs, key_vecs, precision=HIGHEST)
    system = jnp.where(strict, beta_rates[..., :, None] * key_dots * fading, 0.0)
    inverse = unit_lower_inverse(system)
    key_mix = mm(inverse, (beta_rates * jnp.exp(cumulative))[..., None] * key_vecs)
    value_mix = mm(inverse, beta_rates[..., None] * value_vecs)
    query_fade = jnp.exp(cumulative)[..., None] * queries
    scores = jnp.einsum("...ik,...jk->...ij", queries, key_vecs, precision=HIGHEST) * fading
    ending = cumulative[..., -1]
    key_fade = jnp.exp(ending[..., None] - cumulative)[..., None] * key_vecs
    key_width = key_vecs.shape[-1]
    fade_t = jnp.swapaxes(key_fade, -1, -2)
    step_map = ending_eye(jnp.exp(ending), key_width) - mm(fade_t, key_mix)
    step_shift = mm(fade_t, value_mix)
    return (query_fade, scores, key_mix, value_mix), (step_map, step_shift)


def ending_eye(scale, width):
    return scale[..., None, None] * jnp.eye(width, dtype=jnp.float32)


def chunk_prefix(step_map, step_shift):
    chunks = step_map.shape[1]
    width = step_map.shape[-1]
    reach = 1
    while reach < chunks:
        eye = jnp.broadcast_to(
            jnp.eye(width, dtype=jnp.float32), step_map[:, :reach].shape
        )
        prev_map = jnp.concatenate([eye, step_map[:, : chunks - reach]], axis=1)
        prev_shift = jnp.concatenate(
            [jnp.zeros_like(step_shift[:, :reach]), step_shift[:, : chunks - reach]], axis=1
        )
        joined = mm(step_map, jnp.concatenate([prev_map, prev_shift], axis=-1))
        step_map, step_shift = joined[..., :width], joined[..., width:] + step_shift
        reach *= 2
    return step_map, step_shift


def segment_entry(seg_map, seg_shift, axis):
    count, mine = lax.axis_size(axis), lax.axis_index(axis)
    width = seg_map.shape[-1]
    excl_map = jnp.broadcast_to(jnp.eye(width, dtype=jnp.float32), seg_map.shape)
    excl_shift = jnp.zeros_like(seg_shift)
    reach = 1
    while reach < count:
        pairs = [(i, i + reach) for i in range(count - reach)]
        last = reach * 2 >= count
        if last:
            got_shift = lax.ppermute(seg_shift, axis, pairs)
            excl_shift = mm(excl_map, got_shift) + excl_shift
        else:
            got = lax.ppermute(jnp.concatenate([seg_map, seg_shift], axis=-1), axis, pairs)
            has = mine >= reach
            both = mm(jnp.stack([seg_map, excl_map]), got[None])
            seg_shift = both[0, ..., width:] + seg_shift
            excl_shift = both[1, ..., width:] + excl_shift
            excl_map = jnp.where(has, both[1, ..., :width], excl_map)
            seg_map = jnp.where(has, both[0, ..., :width], seg_map)
        reach *= 2
    return excl_shift


def chunk_outputs(parts, chunk_states):
    query_fade, scores, key_mix, value_mix = parts
    new_values = value_mix - mm(key_mix, chunk_states)
    return mm(query_fade, chunk_states) + mm(scores, new_values)


def head_spans(values):
    moved = jnp.moveaxis(values, 1, 0)
    return moved.reshape((moved.shape[0], moved.shape[1] // CH, CH) + moved.shape[2:])


def run_experts(arrived, local_experts, capacity, gate_weight, up_weight, down_weight):
    peers = arrived.shape[0]
    model_width = arrived.shape[2]
    grouped = arrived.reshape(peers, local_experts, capacity, model_width)
    gate_part = jnp.einsum(
        "pecd,edf->pecf", grouped, gate_weight, preferred_element_type=jnp.float32
    )
    up_part = jnp.einsum("pecd,edf->pecf", grouped, up_weight, preferred_element_type=jnp.float32)
    hidden = (jax.nn.silu(gate_part) * up_part).astype(jnp.bfloat16)
    expert_out = jnp.einsum(
        "pecf,efd->pecd", hidden, down_weight, preferred_element_type=jnp.float32
    ).astype(jnp.bfloat16)
    return expert_out.reshape(peers, local_experts * capacity, model_width)


def local(
    tokens,
    in_gain,
    post_gain,
    w_query,
    w_key,
    w_value,
    w_gate_out,
    w_rates,
    conv_query,
    conv_key,
    conv_value,
    decay_rate,
    time_bias,
    head_gain,
    w_out,
    expert_ids,
    route_gates,
    w_expert_gate,
    w_expert_up,
    w_expert_down,
):
    seq_count = lax.axis_size("seq")
    exp_count = lax.axis_size("exp")
    token_rows = tokens.reshape(tokens.shape[1], tokens.shape[2])
    local_rows = token_rows.shape[0]
    model_width = token_rows.shape[1]
    normed = scale_rows(token_rows.astype(jnp.float32), in_gain).astype(jnp.bfloat16)
    rate_logits = jnp.dot(normed, w_rates, preferred_element_type=jnp.float32).astype(jnp.bfloat16)
    block_rows, block_rates = (
        lax.all_gather(normed, "seq", axis=0, tiled=True),
        lax.all_gather(rate_logits, "seq", axis=0, tiled=True),
    )
    seg_rows = block_rows.shape[0]
    query_proj = jnp.dot(block_rows, w_query, preferred_element_type=jnp.float32)
    key_proj = jnp.dot(block_rows, w_key, preferred_element_type=jnp.float32)
    value_proj = jnp.dot(block_rows, w_value, preferred_element_type=jnp.float32)
    gate_proj = jnp.dot(block_rows, w_gate_out, preferred_element_type=jnp.float32)
    lag_rows = conv_query.shape[0] - 1
    own_tail = jnp.concatenate(
        [
            query_proj[seg_rows - lag_rows :],
            key_proj[seg_rows - lag_rows :],
            value_proj[seg_rows - lag_rows :],
        ],
        axis=1,
    )
    prior = lax.ppermute(own_tail, "exp", [(i, i + 1) for i in range(exp_count - 1)])
    query_cols = query_proj.shape[1]
    key_cols = key_proj.shape[1]
    query_conv = causal_conv(query_proj, prior[:, :query_cols], conv_query)
    key_conv = causal_conv(key_proj, prior[:, query_cols : query_cols + key_cols], conv_key)
    value_conv = causal_conv(value_proj, prior[:, query_cols + key_cols :], conv_value)
    key_heads = query_cols // DK
    value_heads = decay_rate.shape[0]
    ratio = value_heads // key_heads
    total_heads = value_heads * seq_count
    queries = jnp.repeat(unit_heads(query_conv, key_heads) * DK ** (-0.5), ratio, axis=1)
    key_vecs = jnp.repeat(unit_heads(key_conv, key_heads), ratio, axis=1)
    value_vecs = value_conv.reshape(seg_rows, value_heads, DV)
    first_head = lax.axis_index("seq") * value_heads
    rate_values = block_rates.astype(jnp.float32)
    beta_rates = jax.nn.sigmoid(lax.dynamic_slice_in_dim(rate_values, first_head, value_heads, 1))
    decays = -decay_rate * jax.nn.softplus(
        lax.dynamic_slice_in_dim(rate_values, total_heads + first_head, value_heads, 1) + time_bias
    )
    parts, (step_map, step_shift) = chunk_parts(
        head_spans(queries),
        head_spans(key_vecs),
        head_spans(value_vecs),
        head_spans(beta_rates),
        head_spans(decays),
    )
    incl_map, incl_shift = chunk_prefix(step_map, step_shift)
    entering = segment_entry(incl_map[:, -1], incl_shift[:, -1], "exp")
    after = mm(incl_map[:, :-1], entering[:, None]) + incl_shift[:, :-1]
    chunk_states = jnp.concatenate([entering[:, None], after], axis=1)
    recurrent = chunk_outputs(parts, chunk_states)
    recurrent = jnp.moveaxis(recurrent.reshape(value_heads, seg_rows, DV), 0, 1)
    gate_heads = gate_proj.reshape(seg_rows, value_heads, DV)
    gated = (
        (scale_rows(recurrent, head_gain) * jax.nn.silu(gate_heads))
        .reshape(seg_rows, value_heads * DV)
        .astype(jnp.bfloat16)
    )
    picked = gated
    attended = lax.psum_scatter(
        jnp.dot(picked, w_out, preferred_element_type=jnp.float32).astype(jnp.bfloat16),
        "seq",
        scatter_dimension=0,
        tiled=True,
    ).astype(jnp.float32)
    residual = (token_rows.astype(jnp.float32) + attended).astype(jnp.bfloat16)
    moe_in = scale_rows(residual.astype(jnp.float32), post_gain).astype(jnp.bfloat16)
    local_experts = w_expert_gate.shape[0]
    devices = seq_count * exp_count
    experts_all = local_experts * devices
    top_count = expert_ids.shape[2]
    capacity = max(2, local_rows * top_count * 6 // (5 * experts_all))
    pair_ids = expert_ids.reshape(-1)
    columns = jnp.arange(experts_all, dtype=jnp.int32)
    onehot = (pair_ids[:, None] == columns[None, :]).astype(jnp.int32)
    earlier = jnp.cumsum(onehot, axis=0) - onehot
    places = jnp.sum(earlier * onehot, axis=1)
    slots = pair_ids * capacity + places
    sources = jnp.arange(pair_ids.shape[0], dtype=jnp.int32) // top_count
    outgoing = (
        jnp.zeros((experts_all * capacity, model_width), jnp.bfloat16)
        .at[slots]
        .set(moe_in[sources])
    )
    slot_count = local_experts * capacity
    arrived = lax.all_to_all(
        outgoing.reshape(devices, slot_count, model_width),
        ("seq", "exp"),
        split_axis=0,
        concat_axis=0,
        tiled=True,
    )
    answers = run_experts(
        arrived, local_experts, capacity, w_expert_gate, w_expert_up, w_expert_down
    )
    returned = lax.all_to_all(answers, ("seq", "exp"), split_axis=0, concat_axis=0, tiled=True)
    picked = returned.reshape(experts_all * capacity, model_width)[slots].reshape(
        local_rows, top_count, model_width
    )
    gates = route_gates.reshape(local_rows, top_count)
    moe_sum = jnp.einsum("tk,tkd->td", gates, picked.astype(jnp.float32), precision=HIGHEST)
    mixed = (residual.astype(jnp.float32) + moe_sum).astype(jnp.bfloat16)
    return mixed.reshape(1, local_rows, model_width)


def solution(mesh):
    in_specs = (
        P("exp", "seq", None),
        P(),
        P(),
        P(None, "seq"),
        P(None, "seq"),
        P(None, "seq"),
        P(None, "seq"),
        P(),
        P(None, "seq"),
        P(None, "seq"),
        P(None, "seq"),
        P("seq"),
        P("seq"),
        P(),
        P("seq", None),
        P("exp", "seq", None),
        P("exp", "seq", None),
        P(("seq", "exp"), None, None),
        P(("seq", "exp"), None, None),
        P(("seq", "exp"), None, None),
    )
    out_specs = P("exp", "seq", None)
    return jax.shard_map(local, mesh=mesh, in_specs=in_specs, out_specs=out_specs, check_vma=False)
```

```python
import jax
import jax.numpy as jnp
from jax import lax
from jax.sharding import PartitionSpec as P

DK = 128
DV = 128
CH = 64


EPSILON = 1e-06
HIGHEST = lax.Precision.HIGHEST


def scale_rows(values, row_gain):
    factor = lax.rsqrt(jnp.mean(values * values, axis=-1, keepdims=True) + EPSILON)
    return values * factor * row_gain


def causal_conv(projected, before, weights):
    taps = weights.shape[0]
    length = projected.shape[0]
    padded = jnp.concatenate([before, projected], axis=0)
    summed = weights[0] * projected
    for lag_index in range(1, taps):
        begin = taps - 1 - lag_index
        summed = summed + weights[lag_index] * padded[begin : begin + length]
    return jax.nn.silu(summed)


def unit_heads(values, head_count):
    shaped = values.reshape(values.shape[0], head_count, values.shape[1] // head_count)
    return shaped * lax.rsqrt(jnp.sum(shaped * shaped, axis=-1, keepdims=True) + EPSILON)


def mm(a, b):
    return jnp.matmul(a, b, precision=HIGHEST)


def unit_lower_inverse(strict_part):
    size = strict_part.shape[-1]
    power = -strict_part
    inverse = jnp.eye(size, dtype=jnp.float32) + power
    reach = 2
    while reach < size:
        power = mm(power, power)
        inverse = inverse + mm(inverse, power)
        reach *= 2
    return inverse


def chunk_parts(queries, key_vecs, value_vecs, beta_rates, decays):
    span_len = queries.shape[-2]
    cumulative = jnp.cumsum(decays, axis=-1)
    lower_mask = jnp.tril(jnp.ones((span_len, span_len), dtype=bool))
    strict = jnp.tril(jnp.ones((span_len, span_len), dtype=bool), -1)
    spread = cumulative[..., :, None] - cumulative[..., None, :]
    fading = jnp.where(lower_mask, jnp.exp(jnp.where(lower_mask, spread, 0.0)), 0.0)
    key_dots = jnp.einsum("...ik,...jk->...ij", key_vecs, key_vecs, precision=HIGHEST)
    system = jnp.where(strict, beta_rates[..., :, None] * key_dots * fading, 0.0)
    inverse = unit_lower_inverse(system)
    key_mix = mm(inverse, (beta_rates * jnp.exp(cumulative))[..., None] * key_vecs)
    value_mix = mm(inverse, beta_rates[..., None] * value_vecs)
    query_fade = jnp.exp(cumulative)[..., None] * queries
    scores = jnp.einsum("...ik,...jk->...ij", queries, key_vecs, precision=HIGHEST) * fading
    ending = cumulative[..., -1]
    key_fade = jnp.exp(ending[..., None] - cumulative)[..., None] * key_vecs
    key_width = key_vecs.shape[-1]
    fade_t = jnp.swapaxes(key_fade, -1, -2)
    step_map = ending_eye(jnp.exp(ending), key_width) - mm(fade_t, key_mix)
    step_shift = mm(fade_t, value_mix)
    return (query_fade, scores, key_mix, value_mix), (step_map, step_shift)


def ending_eye(scale, width):
    return scale[..., None, None] * jnp.eye(width, dtype=jnp.float32)


def segment_entry(seg_map, seg_shift, axis):
    count, mine = lax.axis_size(axis), lax.axis_index(axis)
    width = seg_map.shape[-1]
    excl_map = jnp.broadcast_to(jnp.eye(width, dtype=jnp.float32), seg_map.shape)
    excl_shift = jnp.zeros_like(seg_shift)
    reach = 1
    while reach < count:
        pairs = [(i, i + reach) for i in range(count - reach)]
        last = reach * 2 >= count
        if last:
            got_shift = lax.ppermute(seg_shift, axis, pairs)
            excl_shift = mm(excl_map, got_shift) + excl_shift
        else:
            got = lax.ppermute(jnp.concatenate([seg_map, seg_shift], axis=-1), axis, pairs)
            has = mine >= reach
            both = mm(jnp.stack([seg_map, excl_map]), got[None])
            seg_shift = both[0, ..., width:] + seg_shift
            excl_shift = both[1, ..., width:] + excl_shift
            excl_map = jnp.where(has, both[1, ..., :width], excl_map)
            seg_map = jnp.where(has, both[0, ..., :width], seg_map)
        reach *= 2
    return excl_shift


def tree_compose(step_map, step_shift):
    width = step_map.shape[-1]
    maps = [step_map[:, c] for c in range(step_map.shape[1])]
    shifts = [step_shift[:, c] for c in range(step_shift.shape[1])]
    while len(maps) > 1:
        pairs = len(maps) // 2
        early = jnp.stack(
            [jnp.concatenate([maps[2 * i], shifts[2 * i]], axis=-1) for i in range(pairs)], axis=1
        )
        late_map = jnp.stack([maps[2 * i + 1] for i in range(pairs)], axis=1)
        late_shift = jnp.stack([shifts[2 * i + 1] for i in range(pairs)], axis=1)
        joined = mm(late_map, early)
        new_maps = [joined[:, i, :, :width] for i in range(pairs)]
        new_shifts = [joined[:, i, :, width:] + late_shift[:, i] for i in range(pairs)]
        if len(maps) % 2:
            new_maps.append(maps[-1])
            new_shifts.append(shifts[-1])
        maps, shifts = new_maps, new_shifts
    return maps[0], shifts[0]


def chunk_states_from(entering, step_map, step_shift):
    states = [entering]
    for c in range(step_map.shape[1] - 1):
        states.append(mm(step_map[:, c], states[-1]) + step_shift[:, c])
    return jnp.stack(states, axis=1)


def chunk_outputs(parts, chunk_states):
    query_fade, scores, key_mix, value_mix = parts
    fixed = mm(scores, value_mix)
    reader = query_fade - mm(scores, key_mix)
    return fixed + mm(reader, chunk_states)


def head_spans(values):
    moved = jnp.moveaxis(values, 1, 0)
    return moved.reshape((moved.shape[0], moved.shape[1] // CH, CH) + moved.shape[2:])


def run_experts(arrived, local_experts, capacity, gate_weight, up_weight, down_weight):
    peers = arrived.shape[0]
    model_width = arrived.shape[2]
    grouped = arrived.reshape(peers, local_experts, capacity, model_width)
    gate_part = jnp.einsum(
        "pecd,edf->pecf", grouped, gate_weight, preferred_element_type=jnp.float32
    )
    up_part = jnp.einsum("pecd,edf->pecf", grouped, up_weight, preferred_element_type=jnp.float32)
    hidden = (jax.nn.silu(gate_part) * up_part).astype(jnp.bfloat16)
    expert_out = jnp.einsum(
        "pecf,efd->pecd", hidden, down_weight, preferred_element_type=jnp.float32
    ).astype(jnp.bfloat16)
    return expert_out.reshape(peers, local_experts * capacity, model_width)


def local(
    tokens,
    in_gain,
    post_gain,
    w_query,
    w_key,
    w_value,
    w_gate_out,
    w_rates,
    conv_query,
    conv_key,
    conv_value,
    decay_rate,
    time_bias,
    head_gain,
    w_out,
    expert_ids,
    route_gates,
    w_expert_gate,
    w_expert_up,
    w_expert_down,
):
    seq_count = lax.axis_size("seq")
    exp_count = lax.axis_size("exp")
    token_rows = tokens.reshape(tokens.shape[1], tokens.shape[2])
    local_rows = token_rows.shape[0]
    model_width = token_rows.shape[1]
    normed = scale_rows(token_rows.astype(jnp.float32), in_gain).astype(jnp.bfloat16)
    rate_logits = jnp.dot(normed, w_rates, preferred_element_type=jnp.float32).astype(jnp.bfloat16)
    block_rows, block_rates = (
        lax.all_gather(normed, "seq", axis=0, tiled=True),
        lax.all_gather(rate_logits, "seq", axis=0, tiled=True),
    )
    seg_rows = block_rows.shape[0]
    query_proj = jnp.dot(block_rows, w_query, preferred_element_type=jnp.float32)
    key_proj = jnp.dot(block_rows, w_key, preferred_element_type=jnp.float32)
    value_proj = jnp.dot(block_rows, w_value, preferred_element_type=jnp.float32)
    gate_proj = jnp.dot(block_rows, w_gate_out, preferred_element_type=jnp.float32)
    lag_rows = conv_query.shape[0] - 1
    own_tail = jnp.concatenate(
        [
            query_proj[seg_rows - lag_rows :],
            key_proj[seg_rows - lag_rows :],
            value_proj[seg_rows - lag_rows :],
        ],
        axis=1,
    )
    prior = lax.ppermute(own_tail, "exp", [(i, i + 1) for i in range(exp_count - 1)])
    query_cols = query_proj.shape[1]
    key_cols = key_proj.shape[1]
    query_conv = causal_conv(query_proj, prior[:, :query_cols], conv_query)
    key_conv = causal_conv(key_proj, prior[:, query_cols : query_cols + key_cols], conv_key)
    value_conv = causal_conv(value_proj, prior[:, query_cols + key_cols :], conv_value)
    key_heads = query_cols // DK
    value_heads = decay_rate.shape[0]
    ratio = value_heads // key_heads
    total_heads = value_heads * seq_count
    queries = jnp.repeat(unit_heads(query_conv, key_heads) * DK ** (-0.5), ratio, axis=1)
    key_vecs = jnp.repeat(unit_heads(key_conv, key_heads), ratio, axis=1)
    value_vecs = value_conv.reshape(seg_rows, value_heads, DV)
    first_head = lax.axis_index("seq") * value_heads
    rate_values = block_rates.astype(jnp.float32)
    beta_rates = jax.nn.sigmoid(lax.dynamic_slice_in_dim(rate_values, first_head, value_heads, 1))
    decays = -decay_rate * jax.nn.softplus(
        lax.dynamic_slice_in_dim(rate_values, total_heads + first_head, value_heads, 1) + time_bias
    )
    parts, (step_map, step_shift) = chunk_parts(
        head_spans(queries),
        head_spans(key_vecs),
        head_spans(value_vecs),
        head_spans(beta_rates),
        head_spans(decays),
    )
    seg_map, seg_shift = tree_compose(step_map, step_shift)
    entering = segment_entry(seg_map, seg_shift, "exp")
    chunk_states = chunk_states_from(entering, step_map, step_shift)
    recurrent = chunk_outputs(parts, chunk_states)
    recurrent = jnp.moveaxis(recurrent.reshape(value_heads, seg_rows, DV), 0, 1)
    gate_heads = gate_proj.reshape(seg_rows, value_heads, DV)
    gated = (
        (scale_rows(recurrent, head_gain) * jax.nn.silu(gate_heads))
        .reshape(seg_rows, value_heads * DV)
        .astype(jnp.bfloat16)
    )
    picked = gated
    attended = lax.psum_scatter(
        jnp.dot(picked, w_out, preferred_element_type=jnp.float32).astype(jnp.bfloat16),
        "seq",
        scatter_dimension=0,
        tiled=True,
    ).astype(jnp.float32)
    residual = (token_rows.astype(jnp.float32) + attended).astype(jnp.bfloat16)
    moe_in = scale_rows(residual.astype(jnp.float32), post_gain).astype(jnp.bfloat16)
    local_experts = w_expert_gate.shape[0]
    devices = seq_count * exp_count
    experts_all = local_experts * devices
    top_count = expert_ids.shape[2]
    capacity = max(2, local_rows * top_count * 6 // (5 * experts_all))
    pair_ids = expert_ids.reshape(-1)
    columns = jnp.arange(experts_all, dtype=jnp.int32)
    onehot = (pair_ids[:, None] == columns[None, :]).astype(jnp.int32)
    earlier = jnp.cumsum(onehot, axis=0) - onehot
    places = jnp.sum(earlier * onehot, axis=1)
    slots = pair_ids * capacity + places
    slot_count = local_experts * capacity
    slot_table = slots.reshape(local_rows, top_count)
    slot_grid = jnp.arange(experts_all * capacity, dtype=jnp.int32).reshape(devices, slot_count)
    hits = slot_table[None, None, :, :] == slot_grid[:, :, None, None]
    pick = jnp.any(hits, axis=-1).astype(jnp.bfloat16)
    outgoing = jnp.einsum(
        "dst,tx->dsx", pick, moe_in, preferred_element_type=jnp.float32
    ).astype(jnp.bfloat16)
    arrived = lax.all_to_all(outgoing, ("seq", "exp"), split_axis=0, concat_axis=0, tiled=True)
    answers = run_experts(
        arrived, local_experts, capacity, w_expert_gate, w_expert_up, w_expert_down
    )
    returned = lax.all_to_all(answers, ("seq", "exp"), split_axis=0, concat_axis=0, tiled=True)
    gates = route_gates.reshape(local_rows, top_count)
    weight = jnp.sum(
        jnp.where(hits, gates[None, None, :, :], 0.0), axis=-1
    )
    moe_sum = jnp.einsum(
        "dst,dsx->tx", weight, returned.astype(jnp.float32), precision=HIGHEST
    )
    mixed = (residual.astype(jnp.float32) + moe_sum).astype(jnp.bfloat16)
    return mixed.reshape(1, local_rows, model_width)


def solution(mesh):
    in_specs = (
        P("exp", "seq", None),
        P(),
        P(),
        P(None, "seq"),
        P(None, "seq"),
        P(None, "seq"),
        P(None, "seq"),
        P(),
        P(None, "seq"),
        P(None, "seq"),
        P(None, "seq"),
        P("seq"),
        P("seq"),
        P(),
        P("seq", None),
        P("exp", "seq", None),
        P("exp", "seq", None),
        P(("seq", "exp"), None, None),
        P(("seq", "exp"), None, None),
        P(("seq", "exp"), None, None),
    )
    out_specs = P("exp", "seq", None)
    return jax.shard_map(local, mesh=mesh, in_specs=in_specs, out_specs=out_specs, check_vma=False)
```

```python
import jax
import jax.numpy as jnp
from jax import lax
from jax.sharding import PartitionSpec as P

DK = 128
DV = 128
CH = 64


EPSILON = 1e-06
HIGHEST = lax.Precision.HIGHEST


def scale_rows(values, row_gain):
    factor = lax.rsqrt(jnp.mean(values * values, axis=-1, keepdims=True) + EPSILON)
    return values * factor * row_gain


def causal_conv(projected, before, weights):
    taps = weights.shape[0]
    length = projected.shape[0]
    padded = jnp.concatenate([before, projected], axis=0)
    summed = weights[0] * projected
    for lag_index in range(1, taps):
        begin = taps - 1 - lag_index
        summed = summed + weights[lag_index] * padded[begin : begin + length]
    return jax.nn.silu(summed)


def unit_heads(values, head_count):
    shaped = values.reshape(values.shape[0], head_count, values.shape[1] // head_count)
    return shaped * lax.rsqrt(jnp.sum(shaped * shaped, axis=-1, keepdims=True) + EPSILON)


def mm(a, b):
    return jnp.matmul(a, b, precision=HIGHEST)


def unit_lower_inverse(strict_part):
    size = strict_part.shape[-1]
    power = -strict_part
    inverse = jnp.eye(size, dtype=jnp.float32) + power
    reach = 2
    while reach < size:
        power = mm(power, power)
        inverse = inverse + mm(inverse, power)
        reach *= 2
    return inverse


def chunk_parts(queries, key_vecs, value_vecs, beta_rates, decays):
    span_len = queries.shape[-2]
    cumulative = jnp.cumsum(decays, axis=-1)
    lower_mask = jnp.tril(jnp.ones((span_len, span_len), dtype=bool))
    strict = jnp.tril(jnp.ones((span_len, span_len), dtype=bool), -1)
    spread = cumulative[..., :, None] - cumulative[..., None, :]
    fading = jnp.where(lower_mask, jnp.exp(jnp.where(lower_mask, spread, 0.0)), 0.0)
    key_dots = jnp.einsum("...ik,...jk->...ij", key_vecs, key_vecs, precision=HIGHEST)
    system = jnp.where(strict, beta_rates[..., :, None] * key_dots * fading, 0.0)
    inverse = unit_lower_inverse(system)
    key_mix = mm(inverse, (beta_rates * jnp.exp(cumulative))[..., None] * key_vecs)
    value_mix = mm(inverse, beta_rates[..., None] * value_vecs)
    query_fade = jnp.exp(cumulative)[..., None] * queries
    scores = jnp.einsum("...ik,...jk->...ij", queries, key_vecs, precision=HIGHEST) * fading
    ending = cumulative[..., -1]
    key_fade = jnp.exp(ending[..., None] - cumulative)[..., None] * key_vecs
    key_width = key_vecs.shape[-1]
    fade_t = jnp.swapaxes(key_fade, -1, -2)
    step_map = ending_eye(jnp.exp(ending), key_width) - mm(fade_t, key_mix)
    step_shift = mm(fade_t, value_mix)
    return (query_fade, scores, key_mix, value_mix), (step_map, step_shift)


def ending_eye(scale, width):
    return scale[..., None, None] * jnp.eye(width, dtype=jnp.float32)


def tree_compose(step_map, step_shift):
    maps, shifts = step_map, step_shift
    while maps.shape[1] > 1:
        even = maps.shape[1] // 2 * 2
        late_map = maps[:, 1:even:2]
        joined_map = mm(late_map, maps[:, 0:even:2])
        joined_shift = mm(late_map, shifts[:, 0:even:2]) + shifts[:, 1:even:2]
        if even < maps.shape[1]:
            joined_map = jnp.concatenate([joined_map, maps[:, even:]], axis=1)
            joined_shift = jnp.concatenate([joined_shift, shifts[:, even:]], axis=1)
        maps, shifts = joined_map, joined_shift
    return maps[:, 0], shifts[:, 0]


def segment_entry(seg_map, seg_shift, axis):
    count = lax.axis_size(axis)
    width = seg_map.shape[-1]
    ex_map, ex_shift = None, jnp.zeros_like(seg_shift)
    inc_map, inc_shift = seg_map, seg_shift
    stride = 1
    while stride < count:
        last = stride * 4 >= count
        gaps = [k * stride for k in (1, 2, 3) if k * stride < count]
        got = []
        for gap in gaps:
            pairs = [(i, i + gap) for i in range(count - gap)]
            if last and gap == gaps[-1]:
                got.append((None, lax.ppermute(inc_shift, axis, pairs)))
            else:
                both = lax.ppermute(jnp.concatenate([inc_map, inc_shift], axis=-1), axis, pairs)
                got.append((both[..., :width], both[..., width:]))
        t_map, t_shift = got[-1]
        for g_map, g_shift in reversed(got[:-1]):
            t_shift = mm(g_map, t_shift) + g_shift
            if not last:
                t_map = mm(g_map, t_map)
        if ex_map is None:
            new_shift, new_map = t_shift, t_map
        else:
            new_shift = mm(ex_map, t_shift) + ex_shift
            new_map = None if last else mm(ex_map, t_map)
        if last:
            return new_shift
        ex_map, ex_shift = new_map, new_shift
        joined = mm(seg_map, jnp.concatenate([ex_map, ex_shift], axis=-1))
        inc_map, inc_shift = joined[..., :width], joined[..., width:] + seg_shift
        stride *= 4
    return ex_shift


def chunk_states_from(entering, step_map, step_shift):
    states = [entering]
    for c in range(step_map.shape[1] - 1):
        states.append(mm(step_map[:, c], states[-1]) + step_shift[:, c])
    return jnp.stack(states, axis=1)


def chunk_outputs(parts, chunk_states):
    query_fade, scores, key_mix, value_mix = parts
    fixed = mm(scores, value_mix)
    reader = query_fade - mm(scores, key_mix)
    return fixed + mm(reader, chunk_states)


def head_spans(values):
    moved = jnp.moveaxis(values, 1, 0)
    return moved.reshape((moved.shape[0], moved.shape[1] // CH, CH) + moved.shape[2:])


def exchange_rows(rows):
    devices, slots, width = rows.shape
    piece = 512 if width % 512 == 0 else width
    packed = rows.reshape(devices, slots * width // piece, piece)
    moved = lax.all_to_all(packed, ("seq", "exp"), split_axis=0, concat_axis=0, tiled=True)
    return moved.reshape(devices, slots, width)


def run_experts(arrived, local_experts, capacity, gate_weight, up_weight, down_weight):
    peers = arrived.shape[0]
    model_width = arrived.shape[2]
    grouped = arrived.reshape(peers, local_experts, capacity, model_width)
    gate_part = jnp.einsum(
        "pecd,edf->pecf", grouped, gate_weight, preferred_element_type=jnp.float32
    )
    up_part = jnp.einsum("pecd,edf->pecf", grouped, up_weight, preferred_element_type=jnp.float32)
    hidden = (jax.nn.silu(gate_part) * up_part).astype(jnp.bfloat16)
    expert_out = jnp.einsum(
        "pecf,efd->pecd", hidden, down_weight, preferred_element_type=jnp.float32
    ).astype(jnp.bfloat16)
    return expert_out.reshape(peers, local_experts * capacity, model_width)


def local(
    tokens,
    in_gain,
    post_gain,
    w_query,
    w_key,
    w_value,
    w_gate_out,
    w_rates,
    conv_query,
    conv_key,
    conv_value,
    decay_rate,
    time_bias,
    head_gain,
    w_out,
    expert_ids,
    route_gates,
    w_expert_gate,
    w_expert_up,
    w_expert_down,
):
    seq_count = lax.axis_size("seq")
    exp_count = lax.axis_size("exp")
    token_rows = tokens.reshape(tokens.shape[1], tokens.shape[2])
    local_rows = token_rows.shape[0]
    model_width = token_rows.shape[1]
    normed = scale_rows(token_rows.astype(jnp.float32), in_gain).astype(jnp.bfloat16)
    rate_logits = jnp.dot(normed, w_rates, preferred_element_type=jnp.float32).astype(jnp.bfloat16)
    block_rows, block_rates = (
        lax.all_gather(normed, "seq", axis=0, tiled=True),
        lax.all_gather(rate_logits, "seq", axis=0, tiled=True),
    )
    seg_rows = block_rows.shape[0]
    query_proj = jnp.dot(block_rows, w_query, preferred_element_type=jnp.float32)
    key_proj = jnp.dot(block_rows, w_key, preferred_element_type=jnp.float32)
    value_proj = jnp.dot(block_rows, w_value, preferred_element_type=jnp.float32)
    gate_proj = jnp.dot(block_rows, w_gate_out, preferred_element_type=jnp.float32)
    lag_rows = conv_query.shape[0] - 1
    own_tail = jnp.concatenate(
        [
            query_proj[seg_rows - lag_rows :],
            key_proj[seg_rows - lag_rows :],
            value_proj[seg_rows - lag_rows :],
        ],
        axis=1,
    )
    prior = lax.ppermute(own_tail, "exp", [(i, i + 1) for i in range(exp_count - 1)])
    query_cols = query_proj.shape[1]
    key_cols = key_proj.shape[1]
    query_conv = causal_conv(query_proj, prior[:, :query_cols], conv_query)
    key_conv = causal_conv(key_proj, prior[:, query_cols : query_cols + key_cols], conv_key)
    value_conv = causal_conv(value_proj, prior[:, query_cols + key_cols :], conv_value)
    key_heads = query_cols // DK
    value_heads = decay_rate.shape[0]
    ratio = value_heads // key_heads
    total_heads = value_heads * seq_count
    queries = jnp.repeat(unit_heads(query_conv, key_heads) * DK ** (-0.5), ratio, axis=1)
    key_vecs = jnp.repeat(unit_heads(key_conv, key_heads), ratio, axis=1)
    value_vecs = value_conv.reshape(seg_rows, value_heads, DV)
    first_head = lax.axis_index("seq") * value_heads
    rate_values = block_rates.astype(jnp.float32)
    beta_rates = jax.nn.sigmoid(lax.dynamic_slice_in_dim(rate_values, first_head, value_heads, 1))
    decays = -decay_rate * jax.nn.softplus(
        lax.dynamic_slice_in_dim(rate_values, total_heads + first_head, value_heads, 1) + time_bias
    )
    parts, (step_map, step_shift) = chunk_parts(
        head_spans(queries),
        head_spans(key_vecs),
        head_spans(value_vecs),
        head_spans(beta_rates),
        head_spans(decays),
    )
    seg_map, seg_shift = tree_compose(step_map, step_shift)
    entering = segment_entry(seg_map, seg_shift, "exp")
    chunk_states = chunk_states_from(entering, step_map, step_shift)
    recurrent = chunk_outputs(parts, chunk_states)
    recurrent = jnp.moveaxis(recurrent.reshape(value_heads, seg_rows, DV), 0, 1)
    gate_heads = gate_proj.reshape(seg_rows, value_heads, DV)
    gated = (
        (scale_rows(recurrent, head_gain) * jax.nn.silu(gate_heads))
        .reshape(seg_rows, value_heads * DV)
        .astype(jnp.bfloat16)
    )
    picked = gated
    attended = lax.psum_scatter(
        jnp.dot(picked, w_out, preferred_element_type=jnp.float32).astype(jnp.bfloat16),
        "seq",
        scatter_dimension=0,
        tiled=True,
    ).astype(jnp.float32)
    residual = (token_rows.astype(jnp.float32) + attended).astype(jnp.bfloat16)
    moe_in = scale_rows(residual.astype(jnp.float32), post_gain).astype(jnp.bfloat16)
    local_experts = w_expert_gate.shape[0]
    devices = seq_count * exp_count
    experts_all = local_experts * devices
    top_count = expert_ids.shape[2]
    capacity = max(2, local_rows * top_count * 6 // (5 * experts_all))
    pair_ids = expert_ids.reshape(-1)
    columns = jnp.arange(experts_all, dtype=jnp.int32)
    onehot = (pair_ids[:, None] == columns[None, :]).astype(jnp.int32)
    earlier = jnp.cumsum(onehot, axis=0) - onehot
    places = jnp.sum(earlier * onehot, axis=1)
    slots = pair_ids * capacity + places
    slot_count = local_experts * capacity
    slot_table = slots.reshape(local_rows, top_count)
    slot_grid = jnp.arange(experts_all * capacity, dtype=jnp.int32).reshape(devices, slot_count)
    hits = slot_table[None, None, :, :] == slot_grid[:, :, None, None]
    pick = jnp.any(hits, axis=-1).astype(jnp.bfloat16)
    outgoing = jnp.einsum(
        "dst,tx->dsx", pick, moe_in, preferred_element_type=jnp.float32
    ).astype(jnp.bfloat16)
    arrived = exchange_rows(outgoing)
    answers = run_experts(
        arrived, local_experts, capacity, w_expert_gate, w_expert_up, w_expert_down
    )
    returned = exchange_rows(answers)
    gates = route_gates.reshape(local_rows, top_count)
    weight = jnp.sum(
        jnp.where(hits, gates[None, None, :, :], 0.0), axis=-1
    )
    moe_sum = jnp.einsum(
        "dst,dsx->tx", weight, returned.astype(jnp.float32), precision=HIGHEST
    )
    mixed = (residual.astype(jnp.float32) + moe_sum).astype(jnp.bfloat16)
    return mixed.reshape(1, local_rows, model_width)


def solution(mesh):
    in_specs = (
        P("exp", "seq", None),
        P(),
        P(),
        P(None, "seq"),
        P(None, "seq"),
        P(None, "seq"),
        P(None, "seq"),
        P(),
        P(None, "seq"),
        P(None, "seq"),
        P(None, "seq"),
        P("seq"),
        P("seq"),
        P(),
        P("seq", None),
        P("exp", "seq", None),
        P("exp", "seq", None),
        P(("seq", "exp"), None, None),
        P(("seq", "exp"), None, None),
        P(("seq", "exp"), None, None),
    )
    out_specs = P("exp", "seq", None)
    return jax.shard_map(local, mesh=mesh, in_specs=in_specs, out_specs=out_specs, check_vma=False)
```

```python
import jax
import jax.numpy as jnp
from jax import lax
from jax.sharding import PartitionSpec as P

DK = 128
DV = 128
CH = 64


EPSILON = 1e-06
HIGHEST = lax.Precision.HIGHEST


def scale_rows(values, row_gain):
    factor = lax.rsqrt(jnp.mean(values * values, axis=-1, keepdims=True) + EPSILON)
    return values * factor * row_gain


def causal_conv(projected, before, weights):
    taps = weights.shape[0]
    length = projected.shape[0]
    padded = jnp.concatenate([before, projected], axis=0)
    summed = weights[0] * projected
    for lag_index in range(1, taps):
        begin = taps - 1 - lag_index
        summed = summed + weights[lag_index] * padded[begin : begin + length]
    return jax.nn.silu(summed)


def unit_heads(values, head_count):
    shaped = values.reshape(values.shape[0], head_count, values.shape[1] // head_count)
    return shaped * lax.rsqrt(jnp.sum(shaped * shaped, axis=-1, keepdims=True) + EPSILON)


def mm(a, b):
    return jnp.matmul(a, b, precision=HIGHEST)


def unit_lower_inverse(strict_part):
    size = strict_part.shape[-1]
    power = -strict_part
    inverse = jnp.eye(size, dtype=jnp.float32) + power
    reach = 2
    while reach < size:
        power = mm(power, power)
        inverse = inverse + mm(inverse, power)
        reach *= 2
    return inverse


def chunk_parts(queries, key_vecs, value_vecs, beta_rates, decays):
    span_len = queries.shape[-2]
    cumulative = jnp.cumsum(decays, axis=-1)
    lower_mask = jnp.tril(jnp.ones((span_len, span_len), dtype=bool))
    strict = jnp.tril(jnp.ones((span_len, span_len), dtype=bool), -1)
    spread = cumulative[..., :, None] - cumulative[..., None, :]
    fading = jnp.where(lower_mask, jnp.exp(jnp.where(lower_mask, spread, 0.0)), 0.0)
    key_dots = jnp.einsum("...ik,...jk->...ij", key_vecs, key_vecs, precision=HIGHEST)
    system = jnp.where(strict, beta_rates[..., :, None] * key_dots * fading, 0.0)
    inverse = unit_lower_inverse(system)
    key_mix = mm(inverse, (beta_rates * jnp.exp(cumulative))[..., None] * key_vecs)
    value_mix = mm(inverse, beta_rates[..., None] * value_vecs)
    query_fade = jnp.exp(cumulative)[..., None] * queries
    scores = jnp.einsum("...ik,...jk->...ij", queries, key_vecs, precision=HIGHEST) * fading
    ending = cumulative[..., -1]
    key_fade = jnp.exp(ending[..., None] - cumulative)[..., None] * key_vecs
    key_width = key_vecs.shape[-1]
    fade_t = jnp.swapaxes(key_fade, -1, -2)
    step_map = ending_eye(jnp.exp(ending), key_width) - mm(fade_t, key_mix)
    step_shift = mm(fade_t, value_mix)
    return (query_fade, scores, key_mix, value_mix), (step_map, step_shift)


def ending_eye(scale, width):
    return scale[..., None, None] * jnp.eye(width, dtype=jnp.float32)


def tree_compose(step_map, step_shift):
    maps, shifts = step_map, step_shift
    while maps.shape[1] > 1:
        even = maps.shape[1] // 2 * 2
        late_map = maps[:, 1:even:2]
        joined_map = mm(late_map, maps[:, 0:even:2])
        joined_shift = mm(late_map, shifts[:, 0:even:2]) + shifts[:, 1:even:2]
        if even < maps.shape[1]:
            joined_map = jnp.concatenate([joined_map, maps[:, even:]], axis=1)
            joined_shift = jnp.concatenate([joined_shift, shifts[:, even:]], axis=1)
        maps, shifts = joined_map, joined_shift
    return maps[:, 0], shifts[:, 0]


def segment_entry(seg_map, seg_shift, axis):
    count = lax.axis_size(axis)
    width = seg_map.shape[-1]
    ex_map, ex_shift = None, jnp.zeros_like(seg_shift)
    inc_map, inc_shift = seg_map, seg_shift
    stride = 1
    while stride < count:
        last = stride * 4 >= count
        gaps = [k * stride for k in (1, 2, 3) if k * stride < count]
        got = []
        for gap in gaps:
            pairs = [(i, i + gap) for i in range(count - gap)]
            if last and gap == gaps[-1]:
                got.append((None, lax.ppermute(inc_shift, axis, pairs)))
            else:
                both = lax.ppermute(jnp.concatenate([inc_map, inc_shift], axis=-1), axis, pairs)
                got.append((both[..., :width], both[..., width:]))
        t_map, t_shift = got[-1]
        for g_map, g_shift in reversed(got[:-1]):
            t_shift = mm(g_map, t_shift) + g_shift
            if not last:
                t_map = mm(g_map, t_map)
        if ex_map is None:
            new_shift, new_map = t_shift, t_map
        else:
            new_shift = mm(ex_map, t_shift) + ex_shift
            new_map = None if last else mm(ex_map, t_map)
        if last:
            return new_shift
        ex_map, ex_shift = new_map, new_shift
        joined = mm(seg_map, jnp.concatenate([ex_map, ex_shift], axis=-1))
        inc_map, inc_shift = joined[..., :width], joined[..., width:] + seg_shift
        stride *= 4
    return ex_shift


def chunk_states_from(entering, step_map, step_shift):
    states = [entering]
    for c in range(step_map.shape[1] - 1):
        states.append(mm(step_map[:, c], states[-1]) + step_shift[:, c])
    return jnp.stack(states, axis=1)


def chunk_outputs(parts, chunk_states):
    query_fade, scores, key_mix, value_mix = parts
    fixed = mm(scores, value_mix)
    reader = query_fade - mm(scores, key_mix)
    return fixed + mm(reader, chunk_states)


def head_spans(values):
    moved = jnp.moveaxis(values, 1, 0)
    return moved.reshape((moved.shape[0], moved.shape[1] // CH, CH) + moved.shape[2:])


def row_piece(width):
    return 512 if width % 512 == 0 else width


def exchange_rows(rows):
    devices, slots, width = rows.shape
    piece = row_piece(width)
    packed = rows.reshape(devices, slots * width // piece, piece)
    moved = lax.all_to_all(packed, ("seq", "exp"), split_axis=0, concat_axis=0, tiled=True)
    return moved.reshape(devices, slots, width)


def run_experts(arrived, local_experts, capacity, gate_weight, up_weight, down_weight):
    peers = arrived.shape[0]
    model_width = arrived.shape[2]
    grouped = arrived.reshape(peers, local_experts, capacity, model_width)
    gate_part = jnp.einsum(
        "pecd,edf->pecf", grouped, gate_weight, preferred_element_type=jnp.float32
    )
    up_part = jnp.einsum("pecd,edf->pecf", grouped, up_weight, preferred_element_type=jnp.float32)
    hidden = (jax.nn.silu(gate_part) * up_part).astype(jnp.bfloat16)
    expert_out = jnp.einsum(
        "pecf,efd->pecd", hidden, down_weight, preferred_element_type=jnp.float32
    ).astype(jnp.bfloat16)
    return expert_out.reshape(peers, local_experts * capacity, model_width)


def local(
    tokens,
    in_gain,
    post_gain,
    w_query,
    w_key,
    w_value,
    w_gate_out,
    w_rates,
    conv_query,
    conv_key,
    conv_value,
    decay_rate,
    time_bias,
    head_gain,
    w_out,
    expert_ids,
    route_gates,
    w_expert_gate,
    w_expert_up,
    w_expert_down,
):
    seq_count = lax.axis_size("seq")
    exp_count = lax.axis_size("exp")
    token_rows = tokens.reshape(tokens.shape[1], tokens.shape[2])
    local_rows = token_rows.shape[0]
    model_width = token_rows.shape[1]
    normed = scale_rows(token_rows.astype(jnp.float32), in_gain).astype(jnp.bfloat16)
    rate_logits = jnp.dot(normed, w_rates, preferred_element_type=jnp.float32).astype(jnp.bfloat16)
    block_rows, block_rates = (
        lax.all_gather(normed, "seq", axis=0, tiled=True),
        lax.all_gather(rate_logits, "seq", axis=0, tiled=True),
    )
    seg_rows = block_rows.shape[0]
    query_proj = jnp.dot(block_rows, w_query, preferred_element_type=jnp.float32)
    key_proj = jnp.dot(block_rows, w_key, preferred_element_type=jnp.float32)
    value_proj = jnp.dot(block_rows, w_value, preferred_element_type=jnp.float32)
    gate_proj = jnp.dot(block_rows, w_gate_out, preferred_element_type=jnp.float32)
    lag_rows = conv_query.shape[0] - 1
    own_tail = jnp.concatenate(
        [
            query_proj[seg_rows - lag_rows :],
            key_proj[seg_rows - lag_rows :],
            value_proj[seg_rows - lag_rows :],
        ],
        axis=1,
    )
    prior = lax.ppermute(own_tail, "exp", [(i, i + 1) for i in range(exp_count - 1)])
    query_cols = query_proj.shape[1]
    key_cols = key_proj.shape[1]
    query_conv = causal_conv(query_proj, prior[:, :query_cols], conv_query)
    key_conv = causal_conv(key_proj, prior[:, query_cols : query_cols + key_cols], conv_key)
    value_conv = causal_conv(value_proj, prior[:, query_cols + key_cols :], conv_value)
    key_heads = query_cols // DK
    value_heads = decay_rate.shape[0]
    ratio = value_heads // key_heads
    total_heads = value_heads * seq_count
    queries = jnp.repeat(unit_heads(query_conv, key_heads) * DK ** (-0.5), ratio, axis=1)
    key_vecs = jnp.repeat(unit_heads(key_conv, key_heads), ratio, axis=1)
    value_vecs = value_conv.reshape(seg_rows, value_heads, DV)
    first_head = lax.axis_index("seq") * value_heads
    rate_values = block_rates.astype(jnp.float32)
    beta_rates = jax.nn.sigmoid(lax.dynamic_slice_in_dim(rate_values, first_head, value_heads, 1))
    decays = -decay_rate * jax.nn.softplus(
        lax.dynamic_slice_in_dim(rate_values, total_heads + first_head, value_heads, 1) + time_bias
    )
    parts, (step_map, step_shift) = chunk_parts(
        head_spans(queries),
        head_spans(key_vecs),
        head_spans(value_vecs),
        head_spans(beta_rates),
        head_spans(decays),
    )
    seg_map, seg_shift = tree_compose(step_map, step_shift)
    entering = segment_entry(seg_map, seg_shift, "exp")
    chunk_states = chunk_states_from(entering, step_map, step_shift)
    recurrent = chunk_outputs(parts, chunk_states)
    recurrent = jnp.moveaxis(recurrent.reshape(value_heads, seg_rows, DV), 0, 1)
    gate_heads = gate_proj.reshape(seg_rows, value_heads, DV)
    gated = (
        (scale_rows(recurrent, head_gain) * jax.nn.silu(gate_heads))
        .reshape(seg_rows, value_heads * DV)
        .astype(jnp.bfloat16)
    )
    picked = gated
    attended = lax.psum_scatter(
        jnp.dot(picked, w_out, preferred_element_type=jnp.float32).astype(jnp.bfloat16),
        "seq",
        scatter_dimension=0,
        tiled=True,
    ).astype(jnp.float32)
    residual = (token_rows.astype(jnp.float32) + attended).astype(jnp.bfloat16)
    moe_in = scale_rows(residual.astype(jnp.float32), post_gain).astype(jnp.bfloat16)
    local_experts = w_expert_gate.shape[0]
    devices = seq_count * exp_count
    experts_all = local_experts * devices
    top_count = expert_ids.shape[2]
    capacity = max(2, local_rows * top_count * 6 // (5 * experts_all))
    pair_ids = expert_ids.reshape(-1)
    columns = jnp.arange(experts_all, dtype=jnp.int32)
    onehot = (pair_ids[:, None] == columns[None, :]).astype(jnp.int32)
    earlier = jnp.cumsum(onehot, axis=0) - onehot
    places = jnp.sum(earlier * onehot, axis=1)
    slots = pair_ids * capacity + places
    slot_count = local_experts * capacity
    slot_table = slots.reshape(local_rows, top_count)
    slot_grid = jnp.arange(experts_all * capacity, dtype=jnp.int32).reshape(devices, slot_count)
    hits = slot_table[None, None, :, :] == slot_grid[:, :, None, None]
    piece = row_piece(model_width)
    split = model_width // piece
    out_rows = lax.broadcasted_iota(jnp.int32, (devices * slot_count * split, 1), 0)
    in_cols = lax.broadcasted_iota(jnp.int32, (1, local_rows * split), 1)
    spread_slots = jnp.repeat(slot_table, split, axis=0)
    spread_pick = jnp.any(
        spread_slots[None, :, :] == (out_rows // split)[:, :, None], axis=-1
    ) & (out_rows % split == in_cols % split)
    outgoing = jnp.dot(
        spread_pick.astype(jnp.bfloat16),
        moe_in.reshape(local_rows * split, piece),
        preferred_element_type=jnp.float32,
    ).astype(jnp.bfloat16)
    arrived = lax.all_to_all(
        outgoing.reshape(devices, slot_count * split, piece),
        ("seq", "exp"),
        split_axis=0,
        concat_axis=0,
        tiled=True,
    ).reshape(devices, slot_count, model_width)
    answers = run_experts(
        arrived, local_experts, capacity, w_expert_gate, w_expert_up, w_expert_down
    )
    returned = exchange_rows(answers)
    gates = route_gates.reshape(local_rows, top_count)
    weight = jnp.sum(
        jnp.where(hits, gates[None, None, :, :], 0.0), axis=-1
    )
    moe_sum = jnp.einsum(
        "dst,dsx->tx", weight, returned.astype(jnp.float32), precision=HIGHEST
    )
    mixed = (residual.astype(jnp.float32) + moe_sum).astype(jnp.bfloat16)
    return mixed.reshape(1, local_rows, model_width)


def solution(mesh):
    in_specs = (
        P("exp", "seq", None),
        P(),
        P(),
        P(None, "seq"),
        P(None, "seq"),
        P(None, "seq"),
        P(None, "seq"),
        P(),
        P(None, "seq"),
        P(None, "seq"),
        P(None, "seq"),
        P("seq"),
        P("seq"),
        P(),
        P("seq", None),
        P("exp", "seq", None),
        P("exp", "seq", None),
        P(("seq", "exp"), None, None),
        P(("seq", "exp"), None, None),
        P(("seq", "exp"), None, None),
    )
    out_specs = P("exp", "seq", None)
    return jax.shard_map(local, mesh=mesh, in_specs=in_specs, out_specs=out_specs, check_vma=False)
```

```python
import jax
import jax.numpy as jnp
from jax import lax
from jax.sharding import PartitionSpec as P

DK = 128
DV = 128
CH = 64


EPSILON = 1e-06
HIGHEST = lax.Precision.HIGHEST


def scale_rows(values, row_gain):
    factor = lax.rsqrt(jnp.mean(values * values, axis=-1, keepdims=True) + EPSILON)
    return values * factor * row_gain


def causal_conv(projected, before, weights):
    taps = weights.shape[0]
    length = projected.shape[0]
    padded = jnp.concatenate([before, projected], axis=0)
    summed = weights[0] * projected
    for lag_index in range(1, taps):
        begin = taps - 1 - lag_index
        summed = summed + weights[lag_index] * padded[begin : begin + length]
    return jax.nn.silu(summed)


def unit_heads(values, head_count):
    shaped = values.reshape(values.shape[0], head_count, values.shape[1] // head_count)
    return shaped * lax.rsqrt(jnp.sum(shaped * shaped, axis=-1, keepdims=True) + EPSILON)


def mm(a, b):
    return jnp.matmul(a, b, precision=HIGHEST)


def unit_lower_inverse(strict_part):
    size = strict_part.shape[-1]
    power = -strict_part
    inverse = jnp.eye(size, dtype=jnp.float32) + power
    reach = 2
    while reach < size:
        power = mm(power, power)
        inverse = inverse + mm(inverse, power)
        reach *= 2
    return inverse


def chunk_parts(queries, key_vecs, value_vecs, beta_rates, decays):
    span_len = queries.shape[-2]
    cumulative = jnp.cumsum(decays, axis=-1)
    lower_mask = jnp.tril(jnp.ones((span_len, span_len), dtype=bool))
    strict = jnp.tril(jnp.ones((span_len, span_len), dtype=bool), -1)
    spread = cumulative[..., :, None] - cumulative[..., None, :]
    fading = jnp.where(lower_mask, jnp.exp(jnp.where(lower_mask, spread, 0.0)), 0.0)
    key_dots = jnp.einsum("...ik,...jk->...ij", key_vecs, key_vecs, precision=HIGHEST)
    system = jnp.where(strict, beta_rates[..., :, None] * key_dots * fading, 0.0)
    inverse = unit_lower_inverse(system)
    key_mix = mm(inverse, (beta_rates * jnp.exp(cumulative))[..., None] * key_vecs)
    value_mix = mm(inverse, beta_rates[..., None] * value_vecs)
    query_fade = jnp.exp(cumulative)[..., None] * queries
    scores = jnp.einsum("...ik,...jk->...ij", queries, key_vecs, precision=HIGHEST) * fading
    ending = cumulative[..., -1]
    key_fade = jnp.exp(ending[..., None] - cumulative)[..., None] * key_vecs
    key_width = key_vecs.shape[-1]
    fade_t = jnp.swapaxes(key_fade, -1, -2)
    step_map = ending_eye(jnp.exp(ending), key_width) - mm(fade_t, key_mix)
    step_shift = mm(fade_t, value_mix)
    return (query_fade, scores, key_mix, value_mix), (step_map, step_shift)


def ending_eye(scale, width):
    return scale[..., None, None] * jnp.eye(width, dtype=jnp.float32)


def tree_compose(step_map, step_shift):
    maps, shifts = step_map, step_shift
    while maps.shape[1] > 1:
        even = maps.shape[1] // 2 * 2
        late_map = maps[:, 1:even:2]
        joined_map = mm(late_map, maps[:, 0:even:2])
        joined_shift = mm(late_map, shifts[:, 0:even:2]) + shifts[:, 1:even:2]
        if even < maps.shape[1]:
            joined_map = jnp.concatenate([joined_map, maps[:, even:]], axis=1)
            joined_shift = jnp.concatenate([joined_shift, shifts[:, even:]], axis=1)
        maps, shifts = joined_map, joined_shift
    return maps[:, 0], shifts[:, 0]


def segment_entry(seg_map, seg_shift, axis):
    count = lax.axis_size(axis)
    width = seg_map.shape[-1]
    ex_map, ex_shift = None, jnp.zeros_like(seg_shift)
    inc_map, inc_shift = seg_map, seg_shift
    stride = 1
    while stride < count:
        last = stride * 4 >= count
        gaps = [k * stride for k in (1, 2, 3) if k * stride < count]
        got = []
        for gap in gaps:
            pairs = [(i, i + gap) for i in range(count - gap)]
            if last and gap == gaps[-1]:
                got.append((None, lax.ppermute(inc_shift, axis, pairs)))
            else:
                both = lax.ppermute(jnp.concatenate([inc_map, inc_shift], axis=-1), axis, pairs)
                got.append((both[..., :width], both[..., width:]))
        t_map, t_shift = got[-1]
        for g_map, g_shift in reversed(got[:-1]):
            t_shift = mm(g_map, t_shift) + g_shift
            if not last:
                t_map = mm(g_map, t_map)
        if ex_map is None:
            new_shift, new_map = t_shift, t_map
        else:
            new_shift = mm(ex_map, t_shift) + ex_shift
            new_map = None if last else mm(ex_map, t_map)
        if last:
            return new_shift
        ex_map, ex_shift = new_map, new_shift
        joined = mm(seg_map, jnp.concatenate([ex_map, ex_shift], axis=-1))
        inc_map, inc_shift = joined[..., :width], joined[..., width:] + seg_shift
        stride *= 4
    return ex_shift


def chunk_states_from(entering, step_map, step_shift):
    states = [entering]
    for c in range(step_map.shape[1] - 1):
        states.append(mm(step_map[:, c], states[-1]) + step_shift[:, c])
    return jnp.stack(states, axis=1)


def chunk_outputs(parts, chunk_states):
    query_fade, scores, key_mix, value_mix = parts
    fixed = mm(scores, value_mix)
    reader = query_fade - mm(scores, key_mix)
    return fixed + mm(reader, chunk_states)


def head_spans(values):
    moved = jnp.moveaxis(values, 1, 0)
    return moved.reshape((moved.shape[0], moved.shape[1] // CH, CH) + moved.shape[2:])


def row_piece(width):
    return 512 if width % 512 == 0 else width


def run_experts(packed, local_experts, capacity, gate_weight, up_weight, down_weight):
    peers, rows, piece = packed.shape
    split = rows // (local_experts * capacity)
    grouped = packed.reshape(peers, local_experts, capacity, split, piece)
    hidden_width = gate_weight.shape[2]
    gate_part = jnp.einsum(
        "pecjx,ejxf->pecf",
        grouped,
        gate_weight.reshape(local_experts, split, piece, hidden_width),
        preferred_element_type=jnp.float32,
    )
    up_part = jnp.einsum(
        "pecjx,ejxf->pecf",
        grouped,
        up_weight.reshape(local_experts, split, piece, hidden_width),
        preferred_element_type=jnp.float32,
    )
    hidden = (jax.nn.silu(gate_part) * up_part).astype(jnp.bfloat16)
    expert_out = jnp.einsum(
        "pecf,efjx->pecjx",
        hidden,
        down_weight.reshape(local_experts, hidden_width, split, piece),
        preferred_element_type=jnp.float32,
    ).astype(jnp.bfloat16)
    return expert_out.reshape(peers, rows, piece)


def local(
    tokens,
    in_gain,
    post_gain,
    w_query,
    w_key,
    w_value,
    w_gate_out,
    w_rates,
    conv_query,
    conv_key,
    conv_value,
    decay_rate,
    time_bias,
    head_gain,
    w_out,
    expert_ids,
    route_gates,
    w_expert_gate,
    w_expert_up,
    w_expert_down,
):
    seq_count = lax.axis_size("seq")
    exp_count = lax.axis_size("exp")
    token_rows = tokens.reshape(tokens.shape[1], tokens.shape[2])
    local_rows = token_rows.shape[0]
    model_width = token_rows.shape[1]
    normed = scale_rows(token_rows.astype(jnp.float32), in_gain).astype(jnp.bfloat16)
    rate_logits = jnp.dot(normed, w_rates, preferred_element_type=jnp.float32).astype(jnp.bfloat16)
    block_rows, block_rates = (
        lax.all_gather(normed, "seq", axis=0, tiled=True),
        lax.all_gather(rate_logits, "seq", axis=0, tiled=True),
    )
    seg_rows = block_rows.shape[0]
    query_proj = jnp.dot(block_rows, w_query, preferred_element_type=jnp.float32)
    key_proj = jnp.dot(block_rows, w_key, preferred_element_type=jnp.float32)
    value_proj = jnp.dot(block_rows, w_value, preferred_element_type=jnp.float32)
    gate_proj = jnp.dot(block_rows, w_gate_out, preferred_element_type=jnp.float32)
    lag_rows = conv_query.shape[0] - 1
    own_tail = jnp.concatenate(
        [
            query_proj[seg_rows - lag_rows :],
            key_proj[seg_rows - lag_rows :],
            value_proj[seg_rows - lag_rows :],
        ],
        axis=1,
    )
    prior = lax.ppermute(own_tail, "exp", [(i, i + 1) for i in range(exp_count - 1)])
    query_cols = query_proj.shape[1]
    key_cols = key_proj.shape[1]
    query_conv = causal_conv(query_proj, prior[:, :query_cols], conv_query)
    key_conv = causal_conv(key_proj, prior[:, query_cols : query_cols + key_cols], conv_key)
    value_conv = causal_conv(value_proj, prior[:, query_cols + key_cols :], conv_value)
    key_heads = query_cols // DK
    value_heads = decay_rate.shape[0]
    ratio = value_heads // key_heads
    total_heads = value_heads * seq_count
    queries = jnp.repeat(unit_heads(query_conv, key_heads) * DK ** (-0.5), ratio, axis=1)
    key_vecs = jnp.repeat(unit_heads(key_conv, key_heads), ratio, axis=1)
    value_vecs = value_conv.reshape(seg_rows, value_heads, DV)
    first_head = lax.axis_index("seq") * value_heads
    rate_values = block_rates.astype(jnp.float32)
    beta_rates = jax.nn.sigmoid(lax.dynamic_slice_in_dim(rate_values, first_head, value_heads, 1))
    decays = -decay_rate * jax.nn.softplus(
        lax.dynamic_slice_in_dim(rate_values, total_heads + first_head, value_heads, 1) + time_bias
    )
    parts, (step_map, step_shift) = chunk_parts(
        head_spans(queries),
        head_spans(key_vecs),
        head_spans(value_vecs),
        head_spans(beta_rates),
        head_spans(decays),
    )
    seg_map, seg_shift = tree_compose(step_map, step_shift)
    entering = segment_entry(seg_map, seg_shift, "exp")
    chunk_states = chunk_states_from(entering, step_map, step_shift)
    recurrent = chunk_outputs(parts, chunk_states)
    recurrent = jnp.moveaxis(recurrent.reshape(value_heads, seg_rows, DV), 0, 1)
    gate_heads = gate_proj.reshape(seg_rows, value_heads, DV)
    gated = (
        (scale_rows(recurrent, head_gain) * jax.nn.silu(gate_heads))
        .reshape(seg_rows, value_heads * DV)
        .astype(jnp.bfloat16)
    )
    picked = gated
    attended = lax.psum_scatter(
        jnp.dot(picked, w_out, preferred_element_type=jnp.float32).astype(jnp.bfloat16),
        "seq",
        scatter_dimension=0,
        tiled=True,
    ).astype(jnp.float32)
    residual = (token_rows.astype(jnp.float32) + attended).astype(jnp.bfloat16)
    moe_in = scale_rows(residual.astype(jnp.float32), post_gain).astype(jnp.bfloat16)
    local_experts = w_expert_gate.shape[0]
    devices = seq_count * exp_count
    experts_all = local_experts * devices
    top_count = expert_ids.shape[2]
    capacity = max(2, local_rows * top_count * 6 // (5 * experts_all))
    pair_ids = expert_ids.reshape(-1)
    columns = jnp.arange(experts_all, dtype=jnp.int32)
    onehot = (pair_ids[:, None] == columns[None, :]).astype(jnp.int32)
    earlier = jnp.cumsum(onehot, axis=0) - onehot
    places = jnp.sum(earlier * onehot, axis=1)
    slots = pair_ids * capacity + places
    slot_count = local_experts * capacity
    slot_table = slots.reshape(local_rows, top_count)
    slot_grid = jnp.arange(experts_all * capacity, dtype=jnp.int32).reshape(devices, slot_count)
    hits = slot_table[None, None, :, :] == slot_grid[:, :, None, None]
    piece = row_piece(model_width)
    split = model_width // piece
    out_rows = lax.broadcasted_iota(jnp.int32, (devices * slot_count * split, 1), 0)
    in_cols = lax.broadcasted_iota(jnp.int32, (1, local_rows * split), 1)
    spread_slots = jnp.repeat(slot_table, split, axis=0)
    spread_pick = jnp.any(
        spread_slots[None, :, :] == (out_rows // split)[:, :, None], axis=-1
    ) & (out_rows % split == in_cols % split)
    outgoing = jnp.dot(
        spread_pick.astype(jnp.bfloat16),
        moe_in.reshape(local_rows * split, piece),
        preferred_element_type=jnp.float32,
    ).astype(jnp.bfloat16)
    arrived = lax.all_to_all(
        outgoing.reshape(devices, slot_count * split, piece),
        ("seq", "exp"),
        split_axis=0,
        concat_axis=0,
        tiled=True,
    )
    answers = run_experts(
        arrived, local_experts, capacity, w_expert_gate, w_expert_up, w_expert_down
    )
    returned = lax.all_to_all(
        answers, ("seq", "exp"), split_axis=0, concat_axis=0, tiled=True
    ).reshape(devices, slot_count, model_width)
    gates = route_gates.reshape(local_rows, top_count)
    weight = jnp.sum(
        jnp.where(hits, gates[None, None, :, :], 0.0), axis=-1
    )
    moe_sum = jnp.einsum(
        "dst,dsx->tx", weight, returned.astype(jnp.float32), precision=HIGHEST
    )
    mixed = (residual.astype(jnp.float32) + moe_sum).astype(jnp.bfloat16)
    return mixed.reshape(1, local_rows, model_width)


def solution(mesh):
    in_specs = (
        P("exp", "seq", None),
        P(),
        P(),
        P(None, "seq"),
        P(None, "seq"),
        P(None, "seq"),
        P(None, "seq"),
        P(),
        P(None, "seq"),
        P(None, "seq"),
        P(None, "seq"),
        P("seq"),
        P("seq"),
        P(),
        P("seq", None),
        P("exp", "seq", None),
        P("exp", "seq", None),
        P(("seq", "exp"), None, None),
        P(("seq", "exp"), None, None),
        P(("seq", "exp"), None, None),
    )
    out_specs = P("exp", "seq", None)
    return jax.shard_map(local, mesh=mesh, in_specs=in_specs, out_specs=out_specs, check_vma=False)
```

```python
import jax
import jax.numpy as jnp
from jax import lax
from jax.sharding import PartitionSpec as P

DK = 128
DV = 128
CH = 64


EPSILON = 1e-06
HIGHEST = lax.Precision.HIGHEST


def scale_rows(values, row_gain):
    factor = lax.rsqrt(jnp.mean(values * values, axis=-1, keepdims=True) + EPSILON)
    return values * factor * row_gain


def causal_conv(projected, before, weights):
    taps = weights.shape[0]
    length = projected.shape[0]
    padded = jnp.concatenate([before, projected], axis=0)
    summed = weights[0] * projected
    for lag_index in range(1, taps):
        begin = taps - 1 - lag_index
        summed = summed + weights[lag_index] * padded[begin : begin + length]
    return jax.nn.silu(summed)


def unit_heads(values, head_count):
    shaped = values.reshape(values.shape[0], head_count, values.shape[1] // head_count)
    return shaped * lax.rsqrt(jnp.sum(shaped * shaped, axis=-1, keepdims=True) + EPSILON)


def mm(a, b):
    return jnp.matmul(a, b, precision=HIGHEST)


def unit_lower_inverse(strict_part):
    size = strict_part.shape[-1]
    power = -strict_part
    inverse = jnp.eye(size, dtype=jnp.float32) + power
    reach = 2
    while reach < size:
        power = mm(power, power)
        inverse = inverse + mm(inverse, power)
        reach *= 2
    return inverse


def chunk_parts(queries, key_vecs, value_vecs, beta_rates, decays):
    span_len = queries.shape[-2]
    cumulative = jnp.cumsum(decays, axis=-1)
    lower_mask = jnp.tril(jnp.ones((span_len, span_len), dtype=bool))
    strict = jnp.tril(jnp.ones((span_len, span_len), dtype=bool), -1)
    spread = cumulative[..., :, None] - cumulative[..., None, :]
    fading = jnp.where(lower_mask, jnp.exp(jnp.where(lower_mask, spread, 0.0)), 0.0)
    key_dots = jnp.einsum("...ik,...jk->...ij", key_vecs, key_vecs, precision=HIGHEST)
    system = jnp.where(strict, beta_rates[..., :, None] * key_dots * fading, 0.0)
    inverse = unit_lower_inverse(system)
    key_mix = mm(inverse, (beta_rates * jnp.exp(cumulative))[..., None] * key_vecs)
    value_mix = mm(inverse, beta_rates[..., None] * value_vecs)
    query_fade = jnp.exp(cumulative)[..., None] * queries
    scores = jnp.einsum("...ik,...jk->...ij", queries, key_vecs, precision=HIGHEST) * fading
    ending = cumulative[..., -1]
    key_fade = jnp.exp(ending[..., None] - cumulative)[..., None] * key_vecs
    key_width = key_vecs.shape[-1]
    fade_t = jnp.swapaxes(key_fade, -1, -2)
    step_map = ending_eye(jnp.exp(ending), key_width) - mm(fade_t, key_mix)
    step_shift = mm(fade_t, value_mix)
    return (query_fade, scores, key_mix, value_mix), (step_map, step_shift)


def ending_eye(scale, width):
    return scale[..., None, None] * jnp.eye(width, dtype=jnp.float32)


def tree_compose(step_map, step_shift):
    maps, shifts = step_map, step_shift
    while maps.shape[1] > 1:
        even = maps.shape[1] // 2 * 2
        late_map = maps[:, 1:even:2]
        joined_map = mm(late_map, maps[:, 0:even:2])
        joined_shift = mm(late_map, shifts[:, 0:even:2]) + shifts[:, 1:even:2]
        if even < maps.shape[1]:
            joined_map = jnp.concatenate([joined_map, maps[:, even:]], axis=1)
            joined_shift = jnp.concatenate([joined_shift, shifts[:, even:]], axis=1)
        maps, shifts = joined_map, joined_shift
    return maps[:, 0], shifts[:, 0]


def segment_entry(seg_map, seg_shift, axis):
    count = lax.axis_size(axis)
    width = seg_map.shape[-1]
    ex_map, ex_shift = None, jnp.zeros_like(seg_shift)
    inc_map, inc_shift = seg_map, seg_shift
    stride = 1
    while stride < count:
        last = stride * 4 >= count
        gaps = [k * stride for k in (1, 2, 3) if k * stride < count]
        got = []
        for gap in gaps:
            pairs = [(i, i + gap) for i in range(count - gap)]
            if last and gap == gaps[-1]:
                got.append((None, lax.ppermute(inc_shift, axis, pairs)))
            else:
                both = lax.ppermute(jnp.concatenate([inc_map, inc_shift], axis=-1), axis, pairs)
                got.append((both[..., :width], both[..., width:]))
        t_map, t_shift = got[-1]
        for g_map, g_shift in reversed(got[:-1]):
            t_shift = mm(g_map, t_shift) + g_shift
            if not last:
                t_map = mm(g_map, t_map)
        if ex_map is None:
            new_shift, new_map = t_shift, t_map
        else:
            new_shift = mm(ex_map, t_shift) + ex_shift
            new_map = None if last else mm(ex_map, t_map)
        if last:
            return new_shift
        ex_map, ex_shift = new_map, new_shift
        joined = mm(seg_map, jnp.concatenate([ex_map, ex_shift], axis=-1))
        inc_map, inc_shift = joined[..., :width], joined[..., width:] + seg_shift
        stride *= 4
    return ex_shift


def chunk_states_from(entering, step_map, step_shift):
    states = [entering]
    for c in range(step_map.shape[1] - 1):
        states.append(mm(step_map[:, c], states[-1]) + step_shift[:, c])
    return jnp.stack(states, axis=1)


def chunk_outputs(parts, chunk_states):
    query_fade, scores, key_mix, value_mix = parts
    fixed = mm(scores, value_mix)
    reader = query_fade - mm(scores, key_mix)
    return fixed + mm(reader, chunk_states)


def head_spans(values):
    moved = jnp.moveaxis(values, 1, 0)
    return moved.reshape((moved.shape[0], moved.shape[1] // CH, CH) + moved.shape[2:])


def row_piece(width):
    return 512 if width % 512 == 0 else width


def run_experts(packed, local_experts, capacity, gate_weight, up_weight, down_weight):
    peers, rows, piece = packed.shape
    split = rows // (local_experts * capacity)
    grouped = packed.reshape(peers, local_experts, capacity, split, piece)
    hidden_width = gate_weight.shape[2]
    gate_part = jnp.einsum(
        "pecjx,ejxf->pecf",
        grouped,
        gate_weight.reshape(local_experts, split, piece, hidden_width),
        preferred_element_type=jnp.float32,
    )
    up_part = jnp.einsum(
        "pecjx,ejxf->pecf",
        grouped,
        up_weight.reshape(local_experts, split, piece, hidden_width),
        preferred_element_type=jnp.float32,
    )
    hidden = (jax.nn.silu(gate_part) * up_part).astype(jnp.bfloat16)
    expert_out = jnp.einsum(
        "pecf,efjx->pecjx",
        hidden,
        down_weight.reshape(local_experts, hidden_width, split, piece),
        preferred_element_type=jnp.float32,
    ).astype(jnp.bfloat16)
    return expert_out.reshape(peers, rows, piece)


def local(
    tokens,
    in_gain,
    post_gain,
    w_query,
    w_key,
    w_value,
    w_gate_out,
    w_rates,
    conv_query,
    conv_key,
    conv_value,
    decay_rate,
    time_bias,
    head_gain,
    w_out,
    expert_ids,
    route_gates,
    w_expert_gate,
    w_expert_up,
    w_expert_down,
):
    seq_count = lax.axis_size("seq")
    exp_count = lax.axis_size("exp")
    token_rows = tokens.reshape(tokens.shape[1], tokens.shape[2])
    local_rows = token_rows.shape[0]
    model_width = token_rows.shape[1]
    normed = scale_rows(token_rows.astype(jnp.float32), in_gain).astype(jnp.bfloat16)
    block_rows = lax.all_gather(normed, "seq", axis=0, tiled=True)
    block_rates = jnp.dot(block_rows, w_rates, preferred_element_type=jnp.float32).astype(
        jnp.bfloat16
    )
    seg_rows = block_rows.shape[0]
    query_proj = jnp.dot(block_rows, w_query, preferred_element_type=jnp.float32)
    key_proj = jnp.dot(block_rows, w_key, preferred_element_type=jnp.float32)
    value_proj = jnp.dot(block_rows, w_value, preferred_element_type=jnp.float32)
    gate_proj = jnp.dot(block_rows, w_gate_out, preferred_element_type=jnp.float32)
    lag_rows = conv_query.shape[0] - 1
    own_tail = jnp.concatenate(
        [
            query_proj[seg_rows - lag_rows :],
            key_proj[seg_rows - lag_rows :],
            value_proj[seg_rows - lag_rows :],
        ],
        axis=1,
    )
    prior = lax.ppermute(own_tail, "exp", [(i, i + 1) for i in range(exp_count - 1)])
    query_cols = query_proj.shape[1]
    key_cols = key_proj.shape[1]
    query_conv = causal_conv(query_proj, prior[:, :query_cols], conv_query)
    key_conv = causal_conv(key_proj, prior[:, query_cols : query_cols + key_cols], conv_key)
    value_conv = causal_conv(value_proj, prior[:, query_cols + key_cols :], conv_value)
    key_heads = query_cols // DK
    value_heads = decay_rate.shape[0]
    ratio = value_heads // key_heads
    total_heads = value_heads * seq_count
    queries = jnp.repeat(unit_heads(query_conv, key_heads) * DK ** (-0.5), ratio, axis=1)
    key_vecs = jnp.repeat(unit_heads(key_conv, key_heads), ratio, axis=1)
    value_vecs = value_conv.reshape(seg_rows, value_heads, DV)
    first_head = lax.axis_index("seq") * value_heads
    rate_values = block_rates.astype(jnp.float32)
    beta_rates = jax.nn.sigmoid(lax.dynamic_slice_in_dim(rate_values, first_head, value_heads, 1))
    decays = -decay_rate * jax.nn.softplus(
        lax.dynamic_slice_in_dim(rate_values, total_heads + first_head, value_heads, 1) + time_bias
    )
    parts, (step_map, step_shift) = chunk_parts(
        head_spans(queries),
        head_spans(key_vecs),
        head_spans(value_vecs),
        head_spans(beta_rates),
        head_spans(decays),
    )
    seg_map, seg_shift = tree_compose(step_map, step_shift)
    entering = segment_entry(seg_map, seg_shift, "exp")
    chunk_states = chunk_states_from(entering, step_map, step_shift)
    recurrent = chunk_outputs(parts, chunk_states)
    recurrent = jnp.moveaxis(recurrent.reshape(value_heads, seg_rows, DV), 0, 1)
    gate_heads = gate_proj.reshape(seg_rows, value_heads, DV)
    gated = (
        (scale_rows(recurrent, head_gain) * jax.nn.silu(gate_heads))
        .reshape(seg_rows, value_heads * DV)
        .astype(jnp.bfloat16)
    )
    picked = gated
    attended = lax.psum_scatter(
        jnp.dot(picked, w_out, preferred_element_type=jnp.float32).astype(jnp.bfloat16),
        "seq",
        scatter_dimension=0,
        tiled=True,
    ).astype(jnp.float32)
    residual = (token_rows.astype(jnp.float32) + attended).astype(jnp.bfloat16)
    moe_in = scale_rows(residual.astype(jnp.float32), post_gain).astype(jnp.bfloat16)
    local_experts = w_expert_gate.shape[0]
    devices = seq_count * exp_count
    experts_all = local_experts * devices
    top_count = expert_ids.shape[2]
    capacity = max(2, local_rows * top_count * 6 // (5 * experts_all))
    pair_ids = expert_ids.reshape(-1)
    columns = jnp.arange(experts_all, dtype=jnp.int32)
    onehot = (pair_ids[:, None] == columns[None, :]).astype(jnp.int32)
    earlier = jnp.cumsum(onehot, axis=0) - onehot
    places = jnp.sum(earlier * onehot, axis=1)
    slots = pair_ids * capacity + places
    slot_count = local_experts * capacity
    slot_table = slots.reshape(local_rows, top_count)
    slot_grid = jnp.arange(experts_all * capacity, dtype=jnp.int32).reshape(devices, slot_count)
    hits = slot_table[None, None, :, :] == slot_grid[:, :, None, None]
    piece = row_piece(model_width)
    split = model_width // piece
    out_rows = lax.broadcasted_iota(jnp.int32, (devices * slot_count * split, 1), 0)
    in_cols = lax.broadcasted_iota(jnp.int32, (1, local_rows * split), 1)
    spread_slots = jnp.repeat(slot_table, split, axis=0)
    spread_pick = jnp.any(
        spread_slots[None, :, :] == (out_rows // split)[:, :, None], axis=-1
    ) & (out_rows % split == in_cols % split)
    outgoing = jnp.dot(
        spread_pick.astype(jnp.bfloat16),
        moe_in.reshape(local_rows * split, piece),
        preferred_element_type=jnp.float32,
    ).astype(jnp.bfloat16)
    arrived = lax.all_to_all(
        outgoing.reshape(devices, slot_count * split, piece),
        ("seq", "exp"),
        split_axis=0,
        concat_axis=0,
        tiled=True,
    )
    answers = run_experts(
        arrived, local_experts, capacity, w_expert_gate, w_expert_up, w_expert_down
    )
    returned = lax.all_to_all(
        answers, ("seq", "exp"), split_axis=0, concat_axis=0, tiled=True
    ).reshape(devices, slot_count, model_width)
    gates = route_gates.reshape(local_rows, top_count)
    weight = jnp.sum(
        jnp.where(hits, gates[None, None, :, :], 0.0), axis=-1
    )
    moe_sum = jnp.einsum(
        "dst,dsx->tx", weight, returned.astype(jnp.float32), precision=HIGHEST
    )
    mixed = (residual.astype(jnp.float32) + moe_sum).astype(jnp.bfloat16)
    return mixed.reshape(1, local_rows, model_width)


def solution(mesh):
    in_specs = (
        P("exp", "seq", None),
        P(),
        P(),
        P(None, "seq"),
        P(None, "seq"),
        P(None, "seq"),
        P(None, "seq"),
        P(),
        P(None, "seq"),
        P(None, "seq"),
        P(None, "seq"),
        P("seq"),
        P("seq"),
        P(),
        P("seq", None),
        P("exp", "seq", None),
        P("exp", "seq", None),
        P(("seq", "exp"), None, None),
        P(("seq", "exp"), None, None),
        P(("seq", "exp"), None, None),
    )
    out_specs = P("exp", "seq", None)
    return jax.shard_map(local, mesh=mesh, in_specs=in_specs, out_specs=out_specs, check_vma=False)
```

```python
import jax
import jax.numpy as jnp
from jax import lax
from jax.sharding import PartitionSpec as P

DK = 128
DV = 128
CH = 64


EPSILON = 1e-06
HIGHEST = lax.Precision.HIGHEST


def scale_rows(values, row_gain):
    factor = lax.rsqrt(jnp.mean(values * values, axis=-1, keepdims=True) + EPSILON)
    return values * factor * row_gain


def causal_conv(projected, before, weights):
    taps = weights.shape[0]
    length = projected.shape[0]
    padded = jnp.concatenate([before, projected], axis=0)
    summed = weights[0] * projected
    for lag_index in range(1, taps):
        begin = taps - 1 - lag_index
        summed = summed + weights[lag_index] * padded[begin : begin + length]
    return jax.nn.silu(summed)


def unit_heads(values, head_count):
    shaped = values.reshape(values.shape[0], head_count, values.shape[1] // head_count)
    return shaped * lax.rsqrt(jnp.sum(shaped * shaped, axis=-1, keepdims=True) + EPSILON)


def mm(a, b):
    return jnp.matmul(a, b, precision=HIGHEST)


def unit_lower_inverse(strict_part):
    size = strict_part.shape[-1]
    power = -strict_part
    inverse = jnp.eye(size, dtype=jnp.float32) + power
    reach = 2
    while reach < size:
        power = mm(power, power)
        inverse = inverse + mm(inverse, power)
        reach *= 2
    return inverse


def chunk_parts(queries, key_vecs, value_vecs, beta_rates, decays):
    span_len = queries.shape[-2]
    cumulative = jnp.cumsum(decays, axis=-1)
    lower_mask = jnp.tril(jnp.ones((span_len, span_len), dtype=bool))
    strict = jnp.tril(jnp.ones((span_len, span_len), dtype=bool), -1)
    spread = cumulative[..., :, None] - cumulative[..., None, :]
    fading = jnp.where(lower_mask, jnp.exp(jnp.where(lower_mask, spread, 0.0)), 0.0)
    key_dots = jnp.einsum("...ik,...jk->...ij", key_vecs, key_vecs, precision=HIGHEST)
    system = jnp.where(strict, beta_rates[..., :, None] * key_dots * fading, 0.0)
    inverse = unit_lower_inverse(system)
    key_mix = mm(inverse, (beta_rates * jnp.exp(cumulative))[..., None] * key_vecs)
    value_mix = mm(inverse, beta_rates[..., None] * value_vecs)
    query_fade = jnp.exp(cumulative)[..., None] * queries
    scores = jnp.einsum("...ik,...jk->...ij", queries, key_vecs, precision=HIGHEST) * fading
    ending = cumulative[..., -1]
    key_fade = jnp.exp(ending[..., None] - cumulative)[..., None] * key_vecs
    key_width = key_vecs.shape[-1]
    fade_t = jnp.swapaxes(key_fade, -1, -2)
    step_map = ending_eye(jnp.exp(ending), key_width) - mm(fade_t, key_mix)
    step_shift = mm(fade_t, value_mix)
    return (query_fade, scores, key_mix, value_mix), (step_map, step_shift)


def ending_eye(scale, width):
    return scale[..., None, None] * jnp.eye(width, dtype=jnp.float32)


def tree_compose(step_map, step_shift):
    maps, shifts = step_map, step_shift
    while maps.shape[1] > 1:
        even = maps.shape[1] // 2 * 2
        late_map = maps[:, 1:even:2]
        joined_map = mm(late_map, maps[:, 0:even:2])
        joined_shift = mm(late_map, shifts[:, 0:even:2]) + shifts[:, 1:even:2]
        if even < maps.shape[1]:
            joined_map = jnp.concatenate([joined_map, maps[:, even:]], axis=1)
            joined_shift = jnp.concatenate([joined_shift, shifts[:, even:]], axis=1)
        maps, shifts = joined_map, joined_shift
    return maps[:, 0], shifts[:, 0]


def segment_entry(seg_map, seg_shift, axis):
    count = lax.axis_size(axis)
    width = seg_map.shape[-1]
    ex_map, ex_shift = None, jnp.zeros_like(seg_shift)
    inc_map, inc_shift = seg_map, seg_shift
    stride = 1
    while stride < count:
        last = stride * 4 >= count
        gaps = [k * stride for k in (1, 2, 3) if k * stride < count]
        got = []
        for gap in gaps:
            pairs = [(i, i + gap) for i in range(count - gap)]
            if last and gap == gaps[-1]:
                got.append((None, lax.ppermute(inc_shift, axis, pairs)))
            else:
                both = lax.ppermute(jnp.concatenate([inc_map, inc_shift], axis=-1), axis, pairs)
                got.append((both[..., :width], both[..., width:]))
        t_map, t_shift = got[-1]
        for g_map, g_shift in reversed(got[:-1]):
            t_shift = mm(g_map, t_shift) + g_shift
            if not last:
                t_map = mm(g_map, t_map)
        if ex_map is None:
            new_shift, new_map = t_shift, t_map
        else:
            new_shift = mm(ex_map, t_shift) + ex_shift
            new_map = None if last else mm(ex_map, t_map)
        if last:
            return new_shift
        ex_map, ex_shift = new_map, new_shift
        joined = mm(seg_map, jnp.concatenate([ex_map, ex_shift], axis=-1))
        inc_map, inc_shift = joined[..., :width], joined[..., width:] + seg_shift
        stride *= 4
    return ex_shift


def chunk_states_from(entering, step_map, step_shift):
    states = [entering]
    for c in range(step_map.shape[1] - 1):
        states.append(mm(step_map[:, c], states[-1]) + step_shift[:, c])
    return jnp.stack(states, axis=1)


def chunk_outputs(parts, chunk_states):
    query_fade, scores, key_mix, value_mix = parts
    fixed = mm(scores, value_mix)
    reader = query_fade - mm(scores, key_mix)
    return fixed + mm(reader, chunk_states)


def head_spans(values):
    moved = jnp.moveaxis(values, 1, 0)
    return moved.reshape((moved.shape[0], moved.shape[1] // CH, CH) + moved.shape[2:])


def row_piece(width):
    return 512 if width % 512 == 0 else width


def run_experts(packed, local_experts, capacity, gate_weight, up_weight, down_weight):
    peers, rows, piece = packed.shape
    split = rows // (local_experts * capacity)
    grouped = packed.reshape(peers, local_experts, capacity, split, piece)
    hidden_width = gate_weight.shape[2]
    gate_part = jnp.einsum(
        "pecjx,ejxf->pecf",
        grouped,
        gate_weight.reshape(local_experts, split, piece, hidden_width),
        preferred_element_type=jnp.float32,
    )
    up_part = jnp.einsum(
        "pecjx,ejxf->pecf",
        grouped,
        up_weight.reshape(local_experts, split, piece, hidden_width),
        preferred_element_type=jnp.float32,
    )
    hidden = (jax.nn.silu(gate_part) * up_part).astype(jnp.bfloat16)
    expert_out = jnp.einsum(
        "pecf,efjx->pecjx",
        hidden,
        down_weight.reshape(local_experts, hidden_width, split, piece),
        preferred_element_type=jnp.float32,
    ).astype(jnp.bfloat16)
    return expert_out.reshape(peers, rows, piece)


def local(
    tokens,
    in_gain,
    post_gain,
    w_query,
    w_key,
    w_value,
    w_gate_out,
    w_rates,
    conv_query,
    conv_key,
    conv_value,
    decay_rate,
    time_bias,
    head_gain,
    w_out,
    expert_ids,
    route_gates,
    w_expert_gate,
    w_expert_up,
    w_expert_down,
):
    seq_count = lax.axis_size("seq")
    exp_count = lax.axis_size("exp")
    token_rows = tokens.reshape(tokens.shape[1], tokens.shape[2])
    local_rows = token_rows.shape[0]
    model_width = token_rows.shape[1]
    normed = scale_rows(token_rows.astype(jnp.float32), in_gain).astype(jnp.bfloat16)
    rate_logits = jnp.dot(normed, w_rates, preferred_element_type=jnp.float32).astype(jnp.bfloat16)
    block_rows, block_rates = (
        lax.all_gather(normed, "seq", axis=0, tiled=True),
        lax.all_gather(rate_logits, "seq", axis=0, tiled=True),
    )
    seg_rows = block_rows.shape[0]
    query_proj = jnp.dot(block_rows, w_query, preferred_element_type=jnp.float32)
    key_proj = jnp.dot(block_rows, w_key, preferred_element_type=jnp.float32)
    value_proj = jnp.dot(block_rows, w_value, preferred_element_type=jnp.float32)
    gate_proj = jnp.dot(block_rows, w_gate_out, preferred_element_type=jnp.float32)
    lag_rows = conv_query.shape[0] - 1
    own_tail = jnp.concatenate(
        [
            query_proj[seg_rows - lag_rows :],
            key_proj[seg_rows - lag_rows :],
            value_proj[seg_rows - lag_rows :],
        ],
        axis=1,
    )
    prior = lax.ppermute(own_tail, "exp", [(i, i + 1) for i in range(exp_count - 1)])
    query_cols = query_proj.shape[1]
    key_cols = key_proj.shape[1]
    query_conv = causal_conv(query_proj, prior[:, :query_cols], conv_query)
    key_conv = causal_conv(key_proj, prior[:, query_cols : query_cols + key_cols], conv_key)
    value_conv = causal_conv(value_proj, prior[:, query_cols + key_cols :], conv_value)
    key_heads = query_cols // DK
    value_heads = decay_rate.shape[0]
    ratio = value_heads // key_heads
    total_heads = value_heads * seq_count
    queries = jnp.repeat(unit_heads(query_conv, key_heads) * DK ** (-0.5), ratio, axis=1)
    key_vecs = jnp.repeat(unit_heads(key_conv, key_heads), ratio, axis=1)
    value_vecs = value_conv.reshape(seg_rows, value_heads, DV)
    first_head = lax.axis_index("seq") * value_heads
    rate_values = block_rates.astype(jnp.float32)
    beta_rates = jax.nn.sigmoid(lax.dynamic_slice_in_dim(rate_values, first_head, value_heads, 1))
    decays = -decay_rate * jax.nn.softplus(
        lax.dynamic_slice_in_dim(rate_values, total_heads + first_head, value_heads, 1) + time_bias
    )
    parts, (step_map, step_shift) = chunk_parts(
        head_spans(queries),
        head_spans(key_vecs),
        head_spans(value_vecs),
        head_spans(beta_rates),
        head_spans(decays),
    )
    seg_map, seg_shift = tree_compose(step_map, step_shift)
    entering = segment_entry(seg_map, seg_shift, "exp")
    chunk_states = chunk_states_from(entering, step_map, step_shift)
    recurrent = chunk_outputs(parts, chunk_states)
    recurrent = jnp.moveaxis(recurrent.reshape(value_heads, seg_rows, DV), 0, 1)
    gate_heads = gate_proj.reshape(seg_rows, value_heads, DV)
    gated = (
        (scale_rows(recurrent, head_gain) * jax.nn.silu(gate_heads))
        .reshape(seg_rows, value_heads * DV)
        .astype(jnp.bfloat16)
    )
    picked = gated
    attended = lax.psum_scatter(
        jnp.dot(picked, w_out, preferred_element_type=jnp.float32).astype(jnp.bfloat16),
        "seq",
        scatter_dimension=0,
        tiled=True,
    ).astype(jnp.float32)
    residual = (token_rows.astype(jnp.float32) + attended).astype(jnp.bfloat16)
    moe_in = scale_rows(residual.astype(jnp.float32), post_gain).astype(jnp.bfloat16)
    local_experts = w_expert_gate.shape[0]
    devices = seq_count * exp_count
    experts_all = local_experts * devices
    top_count = expert_ids.shape[2]
    capacity = max(2, local_rows * top_count * 6 // (5 * experts_all))
    pair_ids = expert_ids.reshape(-1)
    columns = jnp.arange(experts_all, dtype=jnp.int32)
    onehot = (pair_ids[:, None] == columns[None, :]).astype(jnp.int32)
    earlier = jnp.cumsum(onehot, axis=0) - onehot
    places = jnp.sum(earlier * onehot, axis=1)
    slots = pair_ids * capacity + places
    slot_count = local_experts * capacity
    slot_table = slots.reshape(local_rows, top_count)
    piece = row_piece(model_width)
    split = model_width // piece
    out_rows = lax.broadcasted_iota(jnp.int32, (devices * slot_count * split, 1), 0)
    in_cols = lax.broadcasted_iota(jnp.int32, (1, local_rows * split), 1)
    spread_slots = jnp.repeat(slot_table, split, axis=0)
    spread_pick = jnp.any(
        spread_slots[None, :, :] == (out_rows // split)[:, :, None], axis=-1
    ) & (out_rows % split == in_cols % split)
    outgoing = jnp.dot(
        spread_pick.astype(jnp.bfloat16),
        moe_in.reshape(local_rows * split, piece),
        preferred_element_type=jnp.float32,
    ).astype(jnp.bfloat16)
    arrived = lax.all_to_all(
        outgoing.reshape(devices, slot_count * split, piece),
        ("seq", "exp"),
        split_axis=0,
        concat_axis=0,
        tiled=True,
    )
    answers = run_experts(
        arrived, local_experts, capacity, w_expert_gate, w_expert_up, w_expert_down
    )
    returned = lax.all_to_all(answers, ("seq", "exp"), split_axis=0, concat_axis=0, tiled=True)
    gates = route_gates.reshape(local_rows, top_count)
    sum_rows = lax.broadcasted_iota(jnp.int32, (local_rows * split, 1), 0)
    sum_cols = lax.broadcasted_iota(jnp.int32, (1, devices * slot_count * split), 1)
    row_slots = jnp.repeat(slot_table, split, axis=0)
    row_gates = jnp.repeat(gates, split, axis=0)
    spread_weight = jnp.sum(
        jnp.where(row_slots[:, None, :] == (sum_cols // split)[:, :, None], row_gates[:, None, :], 0.0),
        axis=-1,
    )
    spread_weight = jnp.where(sum_rows % split == sum_cols % split, spread_weight, 0.0)
    weight_hi = spread_weight.astype(jnp.bfloat16)
    rest = spread_weight - weight_hi.astype(jnp.float32)
    weight_mid = rest.astype(jnp.bfloat16)
    weight_lo = (rest - weight_mid.astype(jnp.float32)).astype(jnp.bfloat16)
    back_rows = returned.reshape(devices * slot_count * split, piece)
    moe_sum = sum(
        jnp.dot(part, back_rows, preferred_element_type=jnp.float32)
        for part in (weight_hi, weight_mid, weight_lo)
    ).reshape(local_rows, model_width)
    mixed = (residual.astype(jnp.float32) + moe_sum).astype(jnp.bfloat16)
    return mixed.reshape(1, local_rows, model_width)


def solution(mesh):
    in_specs = (
        P("exp", "seq", None),
        P(),
        P(),
        P(None, "seq"),
        P(None, "seq"),
        P(None, "seq"),
        P(None, "seq"),
        P(),
        P(None, "seq"),
        P(None, "seq"),
        P(None, "seq"),
        P("seq"),
        P("seq"),
        P(),
        P("seq", None),
        P("exp", "seq", None),
        P("exp", "seq", None),
        P(("seq", "exp"), None, None),
        P(("seq", "exp"), None, None),
        P(("seq", "exp"), None, None),
    )
    out_specs = P("exp", "seq", None)
    return jax.shard_map(local, mesh=mesh, in_specs=in_specs, out_specs=out_specs, check_vma=False)
```

```python
import jax
import jax.numpy as jnp
from jax import lax
from jax.sharding import PartitionSpec as P

DK = 128
DV = 128
CH = 64


EPSILON = 1e-06
HIGHEST = lax.Precision.HIGHEST


def scale_rows(values, row_gain):
    factor = lax.rsqrt(jnp.mean(values * values, axis=-1, keepdims=True) + EPSILON)
    return values * factor * row_gain


def causal_conv(projected, before, weights):
    taps = weights.shape[0]
    length = projected.shape[0]
    padded = jnp.concatenate([before, projected], axis=0)
    summed = weights[0] * projected
    for lag_index in range(1, taps):
        begin = taps - 1 - lag_index
        summed = summed + weights[lag_index] * padded[begin : begin + length]
    return jax.nn.silu(summed)


def unit_heads(values, head_count):
    shaped = values.reshape(values.shape[0], head_count, values.shape[1] // head_count)
    return shaped * lax.rsqrt(jnp.sum(shaped * shaped, axis=-1, keepdims=True) + EPSILON)


def mm(a, b):
    return jnp.matmul(a, b, precision=HIGHEST)


def unit_lower_inverse(strict_part):
    size = strict_part.shape[-1]
    power = -strict_part
    inverse = jnp.eye(size, dtype=jnp.float32) + power
    reach = 2
    while reach < size:
        power = mm(power, power)
        inverse = inverse + mm(inverse, power)
        reach *= 2
    return inverse


def chunk_parts(queries, key_vecs, value_vecs, beta_rates, decays):
    span_len = queries.shape[-2]
    cumulative = jnp.cumsum(decays, axis=-1)
    lower_mask = jnp.tril(jnp.ones((span_len, span_len), dtype=bool))
    strict = jnp.tril(jnp.ones((span_len, span_len), dtype=bool), -1)
    spread = cumulative[..., :, None] - cumulative[..., None, :]
    fading = jnp.where(lower_mask, jnp.exp(jnp.where(lower_mask, spread, 0.0)), 0.0)
    key_dots = jnp.einsum("...ik,...jk->...ij", key_vecs, key_vecs, precision=HIGHEST)
    system = jnp.where(strict, beta_rates[..., :, None] * key_dots * fading, 0.0)
    inverse = unit_lower_inverse(system)
    key_mix = mm(inverse, (beta_rates * jnp.exp(cumulative))[..., None] * key_vecs)
    value_mix = mm(inverse, beta_rates[..., None] * value_vecs)
    query_fade = jnp.exp(cumulative)[..., None] * queries
    scores = jnp.einsum("...ik,...jk->...ij", queries, key_vecs, precision=HIGHEST) * fading
    ending = cumulative[..., -1]
    key_fade = jnp.exp(ending[..., None] - cumulative)[..., None] * key_vecs
    key_width = key_vecs.shape[-1]
    fade_t = jnp.swapaxes(key_fade, -1, -2)
    step_map = ending_eye(jnp.exp(ending), key_width) - mm(fade_t, key_mix)
    step_shift = mm(fade_t, value_mix)
    return (query_fade, scores, key_mix, value_mix), (step_map, step_shift)


def ending_eye(scale, width):
    return scale[..., None, None] * jnp.eye(width, dtype=jnp.float32)


def tree_compose(step_map, step_shift):
    maps, shifts = step_map, step_shift
    while maps.shape[1] > 1:
        even = maps.shape[1] // 2 * 2
        late_map = maps[:, 1:even:2]
        joined_map = mm(late_map, maps[:, 0:even:2])
        joined_shift = mm(late_map, shifts[:, 0:even:2]) + shifts[:, 1:even:2]
        if even < maps.shape[1]:
            joined_map = jnp.concatenate([joined_map, maps[:, even:]], axis=1)
            joined_shift = jnp.concatenate([joined_shift, shifts[:, even:]], axis=1)
        maps, shifts = joined_map, joined_shift
    return maps[:, 0], shifts[:, 0]


def segment_entry(seg_map, seg_shift, axis):
    count = lax.axis_size(axis)
    width = seg_map.shape[-1]
    ex_map, ex_shift = None, jnp.zeros_like(seg_shift)
    inc_map, inc_shift = seg_map, seg_shift
    stride = 1
    while stride < count:
        last = stride * 4 >= count
        gaps = [k * stride for k in (1, 2, 3) if k * stride < count]
        got = []
        for gap in gaps:
            pairs = [(i, i + gap) for i in range(count - gap)]
            if last and gap == gaps[-1]:
                got.append((None, lax.ppermute(inc_shift, axis, pairs)))
            else:
                both = lax.ppermute(jnp.concatenate([inc_map, inc_shift], axis=-1), axis, pairs)
                got.append((both[..., :width], both[..., width:]))
        t_map, t_shift = got[-1]
        for g_map, g_shift in reversed(got[:-1]):
            t_shift = mm(g_map, t_shift) + g_shift
            if not last:
                t_map = mm(g_map, t_map)
        if ex_map is None:
            new_shift, new_map = t_shift, t_map
        else:
            new_shift = mm(ex_map, t_shift) + ex_shift
            new_map = None if last else mm(ex_map, t_map)
        if last:
            return new_shift
        ex_map, ex_shift = new_map, new_shift
        joined = mm(seg_map, jnp.concatenate([ex_map, ex_shift], axis=-1))
        inc_map, inc_shift = joined[..., :width], joined[..., width:] + seg_shift
        stride *= 4
    return ex_shift


def chunk_states_from(entering, step_map, step_shift):
    states = [entering]
    for c in range(step_map.shape[1] - 1):
        states.append(mm(step_map[:, c], states[-1]) + step_shift[:, c])
    return jnp.stack(states, axis=1)


def chunk_outputs(parts, chunk_states):
    query_fade, scores, key_mix, value_mix = parts
    fixed = mm(scores, value_mix)
    reader = query_fade - mm(scores, key_mix)
    return fixed + mm(reader, chunk_states)


def head_spans(values):
    moved = jnp.moveaxis(values, 1, 0)
    return moved.reshape((moved.shape[0], moved.shape[1] // CH, CH) + moved.shape[2:])


def row_piece(width):
    return 512 if width % 512 == 0 else width


def run_experts(packed, local_experts, capacity, gate_weight, up_weight, down_weight):
    peers, rows, piece = packed.shape
    split = rows // (local_experts * capacity)
    grouped = packed.reshape(peers, local_experts, capacity, split, piece)
    hidden_width = gate_weight.shape[2]
    gate_part = jnp.einsum(
        "pecjx,ejxf->pecf",
        grouped,
        gate_weight.reshape(local_experts, split, piece, hidden_width),
        preferred_element_type=jnp.float32,
    )
    up_part = jnp.einsum(
        "pecjx,ejxf->pecf",
        grouped,
        up_weight.reshape(local_experts, split, piece, hidden_width),
        preferred_element_type=jnp.float32,
    )
    hidden = (jax.nn.silu(gate_part) * up_part).astype(jnp.bfloat16)
    expert_out = jnp.einsum(
        "pecf,efjx->pecjx",
        hidden,
        down_weight.reshape(local_experts, hidden_width, split, piece),
        preferred_element_type=jnp.float32,
    ).astype(jnp.bfloat16)
    return expert_out.reshape(peers, rows, piece)


def local(
    tokens,
    in_gain,
    post_gain,
    w_query,
    w_key,
    w_value,
    w_gate_out,
    w_rates,
    conv_query,
    conv_key,
    conv_value,
    decay_rate,
    time_bias,
    head_gain,
    w_out,
    expert_ids,
    route_gates,
    w_expert_gate,
    w_expert_up,
    w_expert_down,
):
    seq_count = lax.axis_size("seq")
    exp_count = lax.axis_size("exp")
    token_rows = tokens.reshape(tokens.shape[1], tokens.shape[2])
    local_rows = token_rows.shape[0]
    model_width = token_rows.shape[1]
    normed = scale_rows(token_rows.astype(jnp.float32), in_gain).astype(jnp.bfloat16)
    rate_logits = jnp.dot(normed, w_rates, preferred_element_type=jnp.float32).astype(jnp.bfloat16)
    block_rows, block_rates = (
        lax.all_gather(normed, "seq", axis=0, tiled=True),
        lax.all_gather(rate_logits, "seq", axis=0, tiled=True),
    )
    seg_rows = block_rows.shape[0]
    query_proj = jnp.dot(block_rows, w_query, preferred_element_type=jnp.float32)
    key_proj = jnp.dot(block_rows, w_key, preferred_element_type=jnp.float32)
    value_proj = jnp.dot(block_rows, w_value, preferred_element_type=jnp.float32)
    gate_proj = jnp.dot(block_rows, w_gate_out, preferred_element_type=jnp.float32)
    lag_rows = conv_query.shape[0] - 1
    own_tail = jnp.concatenate(
        [
            query_proj[seg_rows - lag_rows :],
            key_proj[seg_rows - lag_rows :],
            value_proj[seg_rows - lag_rows :],
        ],
        axis=1,
    )
    prior = lax.ppermute(own_tail, "exp", [(i, i + 1) for i in range(exp_count - 1)])
    query_cols = query_proj.shape[1]
    key_cols = key_proj.shape[1]
    query_conv = causal_conv(query_proj, prior[:, :query_cols], conv_query)
    key_conv = causal_conv(key_proj, prior[:, query_cols : query_cols + key_cols], conv_key)
    value_conv = causal_conv(value_proj, prior[:, query_cols + key_cols :], conv_value)
    key_heads = query_cols // DK
    value_heads = decay_rate.shape[0]
    ratio = value_heads // key_heads
    total_heads = value_heads * seq_count
    queries = jnp.repeat(unit_heads(query_conv, key_heads) * DK ** (-0.5), ratio, axis=1)
    key_vecs = jnp.repeat(unit_heads(key_conv, key_heads), ratio, axis=1)
    value_vecs = value_conv.reshape(seg_rows, value_heads, DV)
    first_head = lax.axis_index("seq") * value_heads
    rate_values = block_rates.astype(jnp.float32)
    beta_rates = jax.nn.sigmoid(lax.dynamic_slice_in_dim(rate_values, first_head, value_heads, 1))
    decays = -decay_rate * jax.nn.softplus(
        lax.dynamic_slice_in_dim(rate_values, total_heads + first_head, value_heads, 1) + time_bias
    )
    parts, (step_map, step_shift) = chunk_parts(
        head_spans(queries),
        head_spans(key_vecs),
        head_spans(value_vecs),
        head_spans(beta_rates),
        head_spans(decays),
    )
    seg_map, seg_shift = tree_compose(step_map, step_shift)
    entering = segment_entry(seg_map, seg_shift, "exp")
    chunk_states = chunk_states_from(entering, step_map, step_shift)
    recurrent = chunk_outputs(parts, chunk_states)
    recurrent = jnp.moveaxis(recurrent.reshape(value_heads, seg_rows, DV), 0, 1)
    gate_heads = gate_proj.reshape(seg_rows, value_heads, DV)
    gated = (
        (scale_rows(recurrent, head_gain) * jax.nn.silu(gate_heads))
        .reshape(seg_rows, value_heads * DV)
        .astype(jnp.bfloat16)
    )
    picked = gated
    attended = lax.psum_scatter(
        jnp.dot(picked, w_out, preferred_element_type=jnp.float32).astype(jnp.bfloat16),
        "seq",
        scatter_dimension=0,
        tiled=True,
    ).astype(jnp.float32)
    residual = (token_rows.astype(jnp.float32) + attended).astype(jnp.bfloat16)
    moe_in = scale_rows(residual.astype(jnp.float32), post_gain).astype(jnp.bfloat16)
    local_experts = w_expert_gate.shape[0]
    devices = seq_count * exp_count
    experts_all = local_experts * devices
    top_count = expert_ids.shape[2]
    capacity = max(2, local_rows * top_count * 6 // (5 * experts_all))
    pair_ids = expert_ids.reshape(-1)
    columns = jnp.arange(experts_all, dtype=jnp.int32)
    onehot = (pair_ids[:, None] == columns[None, :]).astype(jnp.int32)
    earlier = jnp.cumsum(onehot, axis=0) - onehot
    places = jnp.sum(earlier * onehot, axis=1)
    slots = pair_ids * capacity + places
    slot_count = local_experts * capacity
    slot_table = slots.reshape(local_rows, top_count)
    slot_grid = jnp.arange(experts_all * capacity, dtype=jnp.int32).reshape(devices, slot_count)
    hits = slot_table[None, None, :, :] == slot_grid[:, :, None, None]
    piece = row_piece(model_width)
    split = model_width // piece
    out_rows = lax.broadcasted_iota(jnp.int32, (devices * slot_count * split, 1), 0)
    in_cols = lax.broadcasted_iota(jnp.int32, (1, local_rows * split), 1)
    spread_slots = jnp.repeat(slot_table, split, axis=0)
    spread_pick = jnp.any(
        spread_slots[None, :, :] == (out_rows // split)[:, :, None], axis=-1
    ) & (out_rows % split == in_cols % split)
    outgoing = jnp.dot(
        spread_pick.astype(jnp.bfloat16),
        moe_in.reshape(local_rows * split, piece),
        preferred_element_type=jnp.float32,
    ).astype(jnp.bfloat16)
    arrived = lax.all_to_all(
        outgoing.reshape(devices, slot_count * split, piece),
        ("seq", "exp"),
        split_axis=0,
        concat_axis=0,
        tiled=True,
    )
    answers = run_experts(
        arrived, local_experts, capacity, w_expert_gate, w_expert_up, w_expert_down
    )
    returned = lax.all_to_all(
        answers, ("seq", "exp"), split_axis=0, concat_axis=0, tiled=True
    ).reshape(devices, slot_count, model_width)
    gates = route_gates.reshape(local_rows, top_count)
    weight = jnp.sum(
        jnp.where(hits, gates[None, None, :, :], 0.0), axis=-1
    )
    moe_sum = jnp.einsum(
        "dst,dsx->tx", weight, returned.astype(jnp.float32), precision=lax.Precision.HIGH
    )
    mixed = (residual.astype(jnp.float32) + moe_sum).astype(jnp.bfloat16)
    return mixed.reshape(1, local_rows, model_width)


def solution(mesh):
    in_specs = (
        P("exp", "seq", None),
        P(),
        P(),
        P(None, "seq"),
        P(None, "seq"),
        P(None, "seq"),
        P(None, "seq"),
        P(),
        P(None, "seq"),
        P(None, "seq"),
        P(None, "seq"),
        P("seq"),
        P("seq"),
        P(),
        P("seq", None),
        P("exp", "seq", None),
        P("exp", "seq", None),
        P(("seq", "exp"), None, None),
        P(("seq", "exp"), None, None),
        P(("seq", "exp"), None, None),
    )
    out_specs = P("exp", "seq", None)
    return jax.shard_map(local, mesh=mesh, in_specs=in_specs, out_specs=out_specs, check_vma=False)
```
